256 devices in a mesh: sector: 64 (over x_lo, y, z), range: 4 (over x_hi, core).
Axes of the slice: x: 4 (x_hi: 2, x_lo: 2; x = x_hi * 2 + x_lo), y: 4, z: 8, core: 2. Of those that a mesh axis runs over, the one named last changes fastest.
Arguments:
- echo: bfloat16 [16384, 2, 8192], P('sector', None, 'range'), may hold values from -16 to 16
- nav_angles: float32 [1024, 8192], P('sector', 'range'), may hold values from -3.140625 to 3.140625
- owner: int32 [4], replicated, may hold values from 0 to 63
- taps: bfloat16 [4, 32, 2, 128], P(None, 'range'), may hold values from -0.375 to 0.375
- band: int32 [32], P('range'), may hold values from 16 to 64
Outputs:
- image: bfloat16 [16384, 2, 8192], P('sector', None, 'range')
The draws below stay inside these ranges and needn't reach their ends.
All inputs are finite; a program needn't handle non-finite values.
Results may differ from the reference program's by a relative error of at most 0.023.
Values may be sent and summed in bfloat16 or wider, within the bound.
No kernel may reach another device: no remote copies, remote signals or barrier semaphores. Data moves between devices by JAX's collectives and lax.ppermute only.
A program may use at most 128 MiB of HBM per device.

```python
import jax
import jax.numpy as jnp
from jax import lax

RANGE = 8192
RBW = 256
HALO = 64
PHR = 16
STEPS = 4
PULSES = 16384
RBLOCKS = 32
NAVROWS = 1024
N_SECTOR = 64


def draw_echo(key, part):
    base_key = jax.random.fold_in(key, 11)
    first_key = jax.random.fold_in(base_key, 0)
    falloff = 3.0 * jnp.power(0.1, jnp.arange(RANGE, dtype=jnp.float32) / RANGE)
    values = jnp.clip(jax.random.normal(first_key, (PULSES, 2, RANGE), jnp.float32), -5.0, 5.0)
    return (values * falloff[None, None, :]).astype(jnp.bfloat16)


def draw_band(key, part):
    base_key = jax.random.fold_in(key, 23)
    first_key, second_key = jax.random.split(base_key)
    lowest = max(1, HALO // 4)
    widths = jax.random.randint(first_key, (RBLOCKS,), lowest, HALO + 1, dtype=jnp.int32)
    chosen = jax.random.randint(second_key, (), 0, RBLOCKS, dtype=jnp.int32)
    return jnp.where(jnp.arange(RBLOCKS, dtype=jnp.int32) == chosen, HALO, widths).astype(jnp.int32)


def with_ends(values, key, least, largest):
    longest = values.shape.index(max(values.shape))
    spots = []
    for shift in (0, 1):
        where = [jax.random.randint(jax.random.fold_in(key, axis), (), 0, length) for axis, length in enumerate(values.shape)]
        where[longest] = (where[longest] + shift) % values.shape[longest]
        spots.append(tuple(where))
    return values.at[spots[0]].set(least).at[spots[1]].set(largest)


def block_scale(key, extent, cuts, low, high):
    loudness, own = 1.0, jax.random.fold_in(key, 6)
    for axis_at, blocks in cuts:
        draws = jnp.exp(jax.random.uniform(jax.random.fold_in(own, axis_at), (blocks,), jnp.float32, low / len(cuts), high / len(cuts)))
        loudness = loudness * jnp.repeat(draws, extent[axis_at] // blocks).reshape([-1 if axis == axis_at else 1 for axis in range(len(extent))])
    return loudness


def scatter_about(rng, shape, deviation, most, shards=(), kind=jnp.bfloat16):
    values = jax.random.normal(rng, shape, jnp.float32) * deviation
    if len(shards) > 0:
        values = block_scale(rng, shape, shards, -0.22, 0.18) * values
    return jnp.clip(values, min=-most, max=most).astype(kind)


def setup_inputs(seed: int = 0) -> dict:
    arg_keys = jax.random.split(jax.random.key(seed), 6)
    return {
        "echo": draw_echo(jax.random.fold_in(arg_keys[5], 71), 0),
        "nav_angles": jnp.clip(jax.random.uniform(arg_keys[1], (NAVROWS, RANGE), jnp.float32, -3.140625, 3.140625), -3.140625, 3.140625),
        "owner": with_ends(jax.random.randint(arg_keys[2], (STEPS,), 0, N_SECTOR), jax.random.fold_in(arg_keys[2], 1), 0, N_SECTOR - 1).astype(jnp.int32),
        "taps": scatter_about(arg_keys[3], (STEPS, RBLOCKS, 2, 2 * HALO), (4 * HALO) ** -0.5, 0.375, ((1, 4),)),
        "band": draw_band(jax.random.fold_in(arg_keys[5], 71), 0),
    }


def make_taps(taps, band):
    taps_count = taps.shape[-1]
    half_taps = taps_count // 2
    offsets = jnp.arange(taps_count, dtype=jnp.int32) - half_taps
    band_col = band[:, None]
    inside = (offsets[None, :] >= -band_col) & (offsets[None, :] < band_col)
    band_gain = jnp.sqrt(half_taps / band.astype(jnp.float32))
    weighted = taps.astype(jnp.float32) * inside[None, :, None, :].astype(jnp.float32) * band_gain[None, :, None, None]
    return weighted.astype(jnp.bfloat16)

def toeplitz(weights):
    taps_count = weights.shape[-1]
    window = 2 * taps_count
    padded = jnp.concatenate([weights, jnp.zeros(weights.shape[:-1] + (taps_count + 1,), weights.dtype)], axis=-1)
    repeated = jnp.tile(padded, (1,) * (weights.ndim - 1) + (taps_count,))
    return repeated[..., :taps_count * window].reshape(weights.shape[:-1] + (taps_count, window))

def operator(filters_step):
    toep_real = toeplitz(filters_step[:, 0])
    toep_imag = toeplitz(filters_step[:, 1])
    upper_half = jnp.stack([toep_real, -toep_imag], axis=2)
    lower_half = jnp.stack([toep_imag, toep_real], axis=2)
    return jnp.stack([upper_half, lower_half], axis=1)

def phase_turn(current, angles):
    total_rows = current.shape[0]
    phase_count = angles.shape[0]
    width = current.shape[2]
    grouped = current.reshape(total_rows // phase_count, phase_count, 2, width).astype(jnp.float32)
    cosine = jnp.cos(angles)
    sine_values = jnp.sin(angles)
    real_part = grouped[:, :, 0] * cosine - grouped[:, :, 1] * sine_values
    imag_part = grouped[:, :, 0] * sine_values + grouped[:, :, 1] * cosine
    return jnp.stack([real_part, imag_part], axis=2).reshape(total_rows, 2, width).astype(jnp.bfloat16)

def compress(extended, matrix, blocks):
    out_rows = matrix.shape[2]
    total_rows = extended.shape[0] - out_rows
    queries = total_rows // out_rows
    width = extended.shape[2]
    bins = width // blocks
    front_rows = extended[:total_rows].reshape(queries, out_rows, 2, blocks, bins)
    back_rows = extended[out_rows:total_rows + out_rows].reshape(queries, out_rows, 2, blocks, bins)
    windows = jnp.concatenate([front_rows, back_rows], axis=1)
    result = jnp.einsum('bcidj,qjdbr->qicbr', matrix.astype(jnp.float32), windows.astype(jnp.float32))
    return result.reshape(total_rows, 2, width)

def reference(echo, nav_angles, owner, taps, band):
    filters = make_taps(taps, band)
    angles = nav_angles.reshape(N_SECTOR, PHR, RANGE)[owner]
    blocked = echo.reshape(PULSES, 2, RBLOCKS, RBW).transpose(2, 0, 1, 3)
    angle_blocks = angles.reshape(STEPS, PHR, RBLOCKS, RBW).transpose(2, 0, 1, 3)
    filter_blocks = filters.transpose(1, 0, 2, 3)

    def one_block(item):
        current, block_angles, block_filters = item
        result = jnp.zeros((PULSES, 2, RBW), jnp.float32)
        for step in range(STEPS):
            turned = phase_turn(current, block_angles[step])
            extended = jnp.concatenate([turned[-HALO:], turned, turned[:HALO]], axis=0)
            result = compress(extended, operator(block_filters[step][None]), 1)
            current = result.astype(jnp.bfloat16)
        return result
    outputs = lax.map(one_block, (blocked, angle_blocks, filter_blocks))
    energy = lax.optimization_barrier(jnp.sum(outputs * outputs, axis=(0, 2, 3)))
    row_scale = lax.rsqrt(energy / (2.0 * RANGE) + 1e-05)
    scaled = outputs * row_scale[None, :, None, None]
    return scaled.transpose(1, 2, 0, 3).reshape(PULSES, 2, RANGE).astype(jnp.bfloat16)
```

```python
import jax
import jax.numpy as jnp
from jax import lax
from jax.sharding import PartitionSpec as P

RANGE = 8192


def from_root(value, axis, source):
    count = lax.axis_size(axis)
    kept = jnp.where(lax.axis_index(axis) == source, value, 0).astype(value.dtype)
    bit = 1
    while bit < count:
        pairs = [(i, i ^ bit) for i in range(count)]
        kept = kept + lax.ppermute(kept, axis, pairs)
        bit *= 2
    return kept


def padded_2(block, sides, width):
    for axis, dim in sides:
        count = lax.axis_size(axis)
        forward = [(i, i + 1) for i in range(count - 1)]
        forward.append((count - 1, 0))
        backward = [(target, source) for source, target in forward]
        low = lax.ppermute(
            lax.slice_in_dim(block, block.shape[dim] - width, None, axis=dim), axis, forward
        )
        high = lax.ppermute(lax.slice_in_dim(block, 0, width, axis=dim), axis, backward)
        block = jnp.concatenate([low, block, high], axis=dim)
    return block


def make_taps(taps, band):
    taps_count = taps.shape[-1]
    half_taps = taps_count // 2
    offsets = jnp.arange(taps_count, dtype=jnp.int32) - half_taps
    band_col = band[:, None]
    inside = (offsets[None, :] >= -band_col) & (offsets[None, :] < band_col)
    band_gain = jnp.sqrt(half_taps / band.astype(jnp.float32))
    weighted = (
        taps.astype(jnp.float32)
        * inside[None, :, None, :].astype(jnp.float32)
        * band_gain[None, :, None, None]
    )
    return weighted.astype(jnp.bfloat16)


def toeplitz(weights):
    taps_count = weights.shape[-1]
    window = 2 * taps_count
    padded = jnp.concatenate(
        [weights, jnp.zeros(weights.shape[:-1] + (taps_count + 1,), weights.dtype)], axis=-1
    )
    repeated = jnp.tile(padded, (1,) * (weights.ndim - 1) + (taps_count,))
    return repeated[..., : taps_count * window].reshape(weights.shape[:-1] + (taps_count, window))


def operator(filters_step):
    toep_real = toeplitz(filters_step[:, 0])
    toep_imag = toeplitz(filters_step[:, 1])
    upper_half = jnp.stack([toep_real, -toep_imag], axis=2)
    lower_half = jnp.stack([toep_imag, toep_real], axis=2)
    return jnp.stack([upper_half, lower_half], axis=1)


def phase_turn(current, angles):
    total_rows = current.shape[0]
    phase_count = angles.shape[0]
    width = current.shape[2]
    grouped = current.reshape(total_rows // phase_count, phase_count, 2, width).astype(jnp.float32)
    cosine = jnp.cos(angles)
    sine_values = jnp.sin(angles)
    real_part = grouped[:, :, 0] * cosine - grouped[:, :, 1] * sine_values
    imag_part = grouped[:, :, 0] * sine_values + grouped[:, :, 1] * cosine
    return (
        jnp.stack([real_part, imag_part], axis=2).reshape(total_rows, 2, width).astype(jnp.bfloat16)
    )


def compress(extended, matrix, blocks):
    out_rows = matrix.shape[2]
    total_rows = extended.shape[0] - out_rows
    queries = total_rows // out_rows
    width = extended.shape[2]
    bins = width // blocks
    front_rows = extended[:total_rows].reshape(queries, out_rows, 2, blocks, bins)
    back_rows = extended[out_rows : total_rows + out_rows].reshape(
        queries, out_rows, 2, blocks, bins
    )
    windows = jnp.concatenate([front_rows, back_rows], axis=1)
    result = jnp.einsum("bcidj,qjdbr->qicbr", matrix, windows, preferred_element_type=jnp.float32)
    return result.reshape(total_rows, 2, width)


def on_device(echo, nav_angles, owner, taps, band):
    filters = make_taps(taps, band)
    step_count = taps.shape[0]
    half_taps = taps.shape[-1] // 2
    blocks = band.shape[0]
    current = echo
    for step in range(step_count):
        angles = from_root(nav_angles, "sector", owner[step])
        extended = padded_2(phase_turn(current, angles), (("sector", 0),), half_taps)
        result = compress(extended, operator(filters[step]), blocks)
        current = result.astype(jnp.bfloat16)
    energy = lax.psum(jnp.sum(result * result, axis=(1, 2)), "range")
    row_scale = lax.rsqrt(energy / (2.0 * RANGE) + 1e-05)
    return (result * row_scale[:, None, None]).astype(jnp.bfloat16)


def solution(mesh):
    placed = (
        P("sector", None, "range"),
        P("sector", "range"),
        P(),
        P(None, "range", None, None),
        P("range"),
    )
    return jax.shard_map(
        on_device, mesh=mesh, in_specs=placed, out_specs=P("sector", None, "range"), check_vma=False
    )
```

```python
import functools

import jax
import jax.numpy as jnp
from jax import lax
from jax.experimental import pallas as pl
from jax.experimental.pallas import tpu as pltpu
from jax.sharding import PartitionSpec as P

RANGE = 8192


def from_root(value, axis, source):
    count = lax.axis_size(axis)
    kept = jnp.where(lax.axis_index(axis) == source, value, 0).astype(value.dtype)
    bit = 1
    while bit < count:
        pairs = [(i, i ^ bit) for i in range(count)]
        kept = kept + lax.ppermute(kept, axis, pairs)
        bit *= 2
    return kept


def exchange(low_rows, high_rows, axis):
    count = lax.axis_size(axis)
    forward = [(i, (i + 1) % count) for i in range(count)]
    backward = [((i + 1) % count, i) for i in range(count)]
    low = lax.ppermute(high_rows, axis, forward)
    high = lax.ppermute(low_rows, axis, backward)
    return low, high


def make_taps(taps, band):
    taps_count = taps.shape[-1]
    half_taps = taps_count // 2
    offsets = jnp.arange(taps_count, dtype=jnp.int32) - half_taps
    band_col = band[:, None]
    inside = (offsets[None, :] >= -band_col) & (offsets[None, :] < band_col)
    band_gain = jnp.sqrt(half_taps / band.astype(jnp.float32))
    weighted = (
        taps.astype(jnp.float32)
        * inside[None, :, None, :].astype(jnp.float32)
        * band_gain[None, :, None, None]
    )
    return weighted.astype(jnp.bfloat16)


def toeplitz(weights):
    taps_count = weights.shape[-1]
    window = 2 * taps_count
    padded = jnp.concatenate(
        [weights, jnp.zeros(weights.shape[:-1] + (taps_count + 1,), weights.dtype)], axis=-1
    )
    repeated = jnp.tile(padded, (1,) * (weights.ndim - 1) + (taps_count,))
    return repeated[..., : taps_count * window].reshape(weights.shape[:-1] + (taps_count, window))


def operator(filters_step):
    toep_real = toeplitz(filters_step[:, 0])
    toep_imag = toeplitz(filters_step[:, 1])
    upper_half = jnp.stack([toep_real, -toep_imag], axis=2)
    lower_half = jnp.stack([toep_imag, toep_real], axis=2)
    full = jnp.stack([upper_half, lower_half], axis=1)
    blocks, _, rows, _, window = full.shape
    return full.reshape(blocks, 2 * rows, 2 * window)


def turn_rows(re, im, cosine, sine):
    period = cosine.shape[0]
    rows, width = re.shape
    re = re.astype(jnp.float32).reshape(rows // period, period, width)
    im = im.astype(jnp.float32).reshape(rows // period, period, width)
    real_part = re * cosine[None] - im * sine[None]
    imag_part = re * sine[None] + im * cosine[None]
    return (
        real_part.reshape(rows, width).astype(jnp.bfloat16),
        imag_part.reshape(rows, width).astype(jnp.bfloat16),
    )


def step_kernel(x_ref, lo_ref, hi_ref, cos_ref, sin_ref, t_ref, o_ref, re_s, im_s):
    halo = lo_ref.shape[1]
    rows_in = x_ref.shape[1]
    re_t, im_t = turn_rows(x_ref[0], x_ref[1], cos_ref[...], sin_ref[...])
    re_s[0:halo] = lo_ref[0]
    im_s[0:halo] = lo_ref[1]
    re_s[halo : halo + rows_in] = re_t
    im_s[halo : halo + rows_in] = im_t
    re_s[halo + rows_in :] = hi_ref[0]
    im_s[halo + rows_in :] = hi_ref[1]
    matrix = t_ref[0]
    tile = matrix.shape[0] // 2
    window = matrix.shape[1] // 2
    for q in range(rows_in // tile):
        start = q * tile
        acc = jnp.dot(
            matrix[:, :window], re_s[start : start + window], preferred_element_type=jnp.float32
        )
        acc = acc + jnp.dot(
            matrix[:, window:], im_s[start : start + window], preferred_element_type=jnp.float32
        )
        o_ref[0, start : start + tile] = acc[:tile].astype(o_ref.dtype)
        o_ref[1, start : start + tile] = acc[tile:].astype(o_ref.dtype)


def compress_step(x, low, high, cosine, sine, matrix, out_dtype):
    _, rows, width = x.shape
    blocks = matrix.shape[0]
    bins = width // blocks
    halo = low.shape[1]
    period = cosine.shape[0]
    return pl.pallas_call(
        step_kernel,
        grid=(blocks,),
        in_specs=[
            pl.BlockSpec((2, rows, bins), lambda b: (0, 0, b)),
            pl.BlockSpec((2, halo, bins), lambda b: (0, 0, b)),
            pl.BlockSpec((2, halo, bins), lambda b: (0, 0, b)),
            pl.BlockSpec((period, bins), lambda b: (0, b)),
            pl.BlockSpec((period, bins), lambda b: (0, b)),
            pl.BlockSpec((1,) + matrix.shape[1:], lambda b: (b, 0, 0)),
        ],
        out_specs=pl.BlockSpec((2, rows, bins), lambda b: (0, 0, b)),
        out_shape=jax.ShapeDtypeStruct(x.shape, out_dtype),
        scratch_shapes=[
            pltpu.VMEM((rows + 2 * halo, bins), jnp.bfloat16),
            pltpu.VMEM((rows + 2 * halo, bins), jnp.bfloat16),
        ],
        compiler_params=pltpu.CompilerParams(dimension_semantics=("arbitrary",)),
    )(x, low, high, cosine, sine, matrix)


def on_device(echo, nav_angles, owner, taps, band):
    filters = make_taps(taps, band)
    step_count = taps.shape[0]
    halo = taps.shape[-1] // 2
    current = jnp.transpose(echo, (1, 0, 2))
    rows = current.shape[1]
    result = None
    for step in range(step_count):
        angles = from_root(nav_angles, "sector", owner[step])
        cosine = jnp.cos(angles)
        sine = jnp.sin(angles)
        low_re, low_im = turn_rows(current[0, :halo], current[1, :halo], cosine, sine)
        high_re, high_im = turn_rows(current[0, rows - halo :], current[1, rows - halo :], cosine, sine)
        low, high = exchange(
            jnp.stack([low_re, low_im]), jnp.stack([high_re, high_im]), "sector"
        )
        last = step == step_count - 1
        result = compress_step(
            current, low, high, cosine, sine, operator(filters[step]),
            jnp.float32 if last else jnp.bfloat16,
        )
        current = result
    energy = lax.psum(jnp.sum(result * result, axis=(0, 2)), "range")
    row_scale = lax.rsqrt(energy / (2.0 * RANGE) + 1e-05)
    scaled = (result * row_scale[None, :, None]).astype(jnp.bfloat16)
    return jnp.transpose(scaled, (1, 0, 2))


def solution(mesh):
    placed = (
        P("sector", None, "range"),
        P("sector", "range"),
        P(),
        P(None, "range", None, None),
        P("range"),
    )
    return jax.shard_map(
        on_device, mesh=mesh, in_specs=placed, out_specs=P("sector", None, "range"), check_vma=False
    )
```

```python
import functools

import jax
import jax.numpy as jnp
from jax import lax
from jax.experimental import pallas as pl
from jax.experimental.pallas import tpu as pltpu
from jax.sharding import PartitionSpec as P

RANGE = 8192


def from_root(value, axis, source):
    count = lax.axis_size(axis)
    kept = jnp.where(lax.axis_index(axis) == source, value, 0).astype(value.dtype)
    bit = 1
    while bit < count:
        pairs = [(i, i ^ bit) for i in range(count)]
        kept = kept + lax.ppermute(kept, axis, pairs)
        bit *= 2
    return kept


def exchange(low_rows, high_rows, axis):
    count = lax.axis_size(axis)
    forward = [(i, (i + 1) % count) for i in range(count)]
    backward = [((i + 1) % count, i) for i in range(count)]
    low = lax.ppermute(high_rows, axis, forward)
    high = lax.ppermute(low_rows, axis, backward)
    return low, high


def make_taps(taps, band):
    taps_count = taps.shape[-1]
    half_taps = taps_count // 2
    offsets = jnp.arange(taps_count, dtype=jnp.int32) - half_taps
    band_col = band[:, None]
    inside = (offsets[None, :] >= -band_col) & (offsets[None, :] < band_col)
    band_gain = jnp.sqrt(half_taps / band.astype(jnp.float32))
    weighted = (
        taps.astype(jnp.float32)
        * inside[None, :, None, :].astype(jnp.float32)
        * band_gain[None, :, None, None]
    )
    return weighted.astype(jnp.bfloat16)


def turn_rows(re, im, cosine, sine):
    period = cosine.shape[0]
    rows, width = re.shape
    re = re.astype(jnp.float32).reshape(rows // period, period, width)
    im = im.astype(jnp.float32).reshape(rows // period, period, width)
    real_part = re * cosine[None] - im * sine[None]
    imag_part = re * sine[None] + im * cosine[None]
    return (
        real_part.reshape(rows, width).astype(jnp.bfloat16),
        imag_part.reshape(rows, width).astype(jnp.bfloat16),
    )


def toeplitz_rows(weights, window):
    taps = weights.shape[-1]
    base = jnp.concatenate(
        [jnp.broadcast_to(weights, (taps, taps)), jnp.zeros((taps, window - taps), weights.dtype)],
        axis=1,
    )
    return pltpu.roll(base, 0, 1, stride=1, stride_axis=0)


def step_kernel(x_ref, lo_ref, hi_ref, cos_ref, sin_ref, f_ref, o_ref, re_s, im_s):
    halo = lo_ref.shape[1]
    rows_in = x_ref.shape[1]
    re_t, im_t = turn_rows(x_ref[0], x_ref[1], cos_ref[...], sin_ref[...])
    re_s[0:halo] = lo_ref[0]
    im_s[0:halo] = lo_ref[1]
    re_s[halo : halo + rows_in] = re_t
    im_s[halo : halo + rows_in] = im_t
    re_s[halo + rows_in :] = hi_ref[0]
    im_s[halo + rows_in :] = hi_ref[1]
    weights = f_ref[0]
    tile = weights.shape[-1]
    window = 2 * tile
    toep_real = toeplitz_rows(weights[0:1], window)
    toep_imag = toeplitz_rows(weights[1:2], window)
    from_real = jnp.concatenate([toep_real, toep_imag], axis=0).astype(jnp.bfloat16)
    from_imag = jnp.concatenate([-toep_imag, toep_real], axis=0).astype(jnp.bfloat16)
    for q in range(rows_in // tile):
        start = q * tile
        acc = jnp.dot(from_real, re_s[start : start + window], preferred_element_type=jnp.float32)
        acc = acc + jnp.dot(
            from_imag, im_s[start : start + window], preferred_element_type=jnp.float32
        )
        o_ref[0, start : start + tile] = acc[:tile].astype(o_ref.dtype)
        o_ref[1, start : start + tile] = acc[tile:].astype(o_ref.dtype)


def compress_step(x, low, high, cosine, sine, weights, out_dtype):
    _, rows, width = x.shape
    blocks = weights.shape[0]
    bins = width // blocks
    halo = low.shape[1]
    period = cosine.shape[0]
    return pl.pallas_call(
        step_kernel,
        grid=(blocks,),
        in_specs=[
            pl.BlockSpec((2, rows, bins), lambda b: (0, 0, b)),
            pl.BlockSpec((2, halo, bins), lambda b: (0, 0, b)),
            pl.BlockSpec((2, halo, bins), lambda b: (0, 0, b)),
            pl.BlockSpec((period, bins), lambda b: (0, b)),
            pl.BlockSpec((period, bins), lambda b: (0, b)),
            pl.BlockSpec((1,) + weights.shape[1:], lambda b: (b, 0, 0)),
        ],
        out_specs=pl.BlockSpec((2, rows, bins), lambda b: (0, 0, b)),
        out_shape=jax.ShapeDtypeStruct(x.shape, out_dtype),
        scratch_shapes=[
            pltpu.VMEM((rows + 2 * halo, bins), jnp.bfloat16),
            pltpu.VMEM((rows + 2 * halo, bins), jnp.bfloat16),
        ],
        compiler_params=pltpu.CompilerParams(dimension_semantics=("arbitrary",)),
    )(x, low, high, cosine, sine, weights)


def on_device(echo, nav_angles, owner, taps, band):
    filters = make_taps(taps, band).astype(jnp.float32)
    step_count = taps.shape[0]
    halo = taps.shape[-1] // 2
    current = jnp.transpose(echo, (1, 0, 2))
    rows = current.shape[1]
    result = None
    for step in range(step_count):
        angles = from_root(nav_angles, "sector", owner[step])
        cosine = jnp.cos(angles)
        sine = jnp.sin(angles)
        low_re, low_im = turn_rows(current[0, :halo], current[1, :halo], cosine, sine)
        high_re, high_im = turn_rows(current[0, rows - halo :], current[1, rows - halo :], cosine, sine)
        low, high = exchange(
            jnp.stack([low_re, low_im]), jnp.stack([high_re, high_im]), "sector"
        )
        last = step == step_count - 1
        result = compress_step(
            current, low, high, cosine, sine, filters[step],
            jnp.float32 if last else jnp.bfloat16,
        )
        current = result
    energy = lax.psum(jnp.sum(result * result, axis=(0, 2)), "range")
    row_scale = lax.rsqrt(energy / (2.0 * RANGE) + 1e-05)
    scaled = (result * row_scale[None, :, None]).astype(jnp.bfloat16)
    return jnp.transpose(scaled, (1, 0, 2))


def solution(mesh):
    placed = (
        P("sector", None, "range"),
        P("sector", "range"),
        P(),
        P(None, "range", None, None),
        P("range"),
    )
    return jax.shard_map(
        on_device, mesh=mesh, in_specs=placed, out_specs=P("sector", None, "range"), check_vma=False
    )
```

```python
import functools

import jax
import jax.numpy as jnp
from jax import lax
from jax.experimental import pallas as pl
from jax.experimental.pallas import tpu as pltpu
from jax.sharding import PartitionSpec as P

RANGE = 8192


def from_root(value, axis, source):
    count = lax.axis_size(axis)
    kept = jnp.where(lax.axis_index(axis) == source, value, 0).astype(value.dtype)
    bit = 1
    while bit < count:
        pairs = [(i, i ^ bit) for i in range(count)]
        kept = kept + lax.ppermute(kept, axis, pairs)
        bit *= 2
    return kept


def exchange(low_rows, high_rows, axis):
    count = lax.axis_size(axis)
    forward = [(i, (i + 1) % count) for i in range(count)]
    backward = [((i + 1) % count, i) for i in range(count)]
    low = lax.ppermute(high_rows, axis, forward)
    high = lax.ppermute(low_rows, axis, backward)
    return low, high


def make_taps(taps, band):
    taps_count = taps.shape[-1]
    half_taps = taps_count // 2
    offsets = jnp.arange(taps_count, dtype=jnp.int32) - half_taps
    band_col = band[:, None]
    inside = (offsets[None, :] >= -band_col) & (offsets[None, :] < band_col)
    band_gain = jnp.sqrt(half_taps / band.astype(jnp.float32))
    weighted = (
        taps.astype(jnp.float32)
        * inside[None, :, None, :].astype(jnp.float32)
        * band_gain[None, :, None, None]
    )
    return weighted.astype(jnp.bfloat16)


def turn_rows(re, im, cosine, sine):
    period = cosine.shape[0]
    rows, width = re.shape
    re = re.astype(jnp.float32).reshape(rows // period, period, width)
    im = im.astype(jnp.float32).reshape(rows // period, period, width)
    real_part = re * cosine[None] - im * sine[None]
    imag_part = re * sine[None] + im * cosine[None]
    return (
        real_part.reshape(rows, width).astype(jnp.bfloat16),
        imag_part.reshape(rows, width).astype(jnp.bfloat16),
    )


def toeplitz_rows(weights, window):
    taps = weights.shape[-1]
    base = jnp.concatenate(
        [jnp.broadcast_to(weights, (taps, taps)), jnp.zeros((taps, window - taps), weights.dtype)],
        axis=1,
    )
    return pltpu.roll(base, 0, 1, stride=1, stride_axis=0)


def step_kernel(*refs):
    *pieces, cos_ref, sin_ref, f_ref, o_ref, re_s, im_s = refs
    offset = 0
    for piece in pieces:
        rows = piece.shape[1]
        re_t, im_t = turn_rows(piece[0], piece[1], cos_ref[...], sin_ref[...])
        re_s[offset : offset + rows] = re_t
        im_s[offset : offset + rows] = im_t
        offset += rows
    weights = f_ref[0]
    tile = weights.shape[-1]
    window = 2 * tile
    toep_real = toeplitz_rows(weights[0:1], window)
    toep_imag = toeplitz_rows(weights[1:2], window)
    from_real = jnp.concatenate([toep_real, toep_imag], axis=0).astype(jnp.bfloat16)
    from_imag = jnp.concatenate([-toep_imag, toep_real], axis=0).astype(jnp.bfloat16)
    for q in range(offset // tile - 1):
        start = q * tile
        acc = jnp.dot(from_real, re_s[start : start + window], preferred_element_type=jnp.float32)
        acc = acc + jnp.dot(
            from_imag, im_s[start : start + window], preferred_element_type=jnp.float32
        )
        o_ref[0, start : start + tile] = acc[:tile].astype(o_ref.dtype)
        o_ref[1, start : start + tile] = acc[tile:].astype(o_ref.dtype)


def compress_step(pieces, cosine, sine, weights, out_dtype):
    width = pieces[0].shape[2]
    rows = sum(piece.shape[1] for piece in pieces)
    blocks = weights.shape[0]
    bins = width // blocks
    period = cosine.shape[0]
    out_rows = rows - weights.shape[-1]
    return pl.pallas_call(
        step_kernel,
        grid=(blocks,),
        in_specs=[pl.BlockSpec((2, piece.shape[1], bins), lambda b: (0, 0, b)) for piece in pieces]
        + [
            pl.BlockSpec((period, bins), lambda b: (0, b)),
            pl.BlockSpec((period, bins), lambda b: (0, b)),
            pl.BlockSpec((1,) + weights.shape[1:], lambda b: (b, 0, 0)),
        ],
        out_specs=pl.BlockSpec((2, out_rows, bins), lambda b: (0, 0, b)),
        out_shape=jax.ShapeDtypeStruct((2, out_rows, width), out_dtype),
        scratch_shapes=[
            pltpu.VMEM((rows, bins), jnp.bfloat16),
            pltpu.VMEM((rows, bins), jnp.bfloat16),
        ],
        compiler_params=pltpu.CompilerParams(dimension_semantics=("arbitrary",)),
    )(*pieces, cosine, sine, weights)


def on_device(echo, nav_angles, owner, taps, band):
    filters = make_taps(taps, band).astype(jnp.float32)
    step_count = taps.shape[0]
    own = jnp.transpose(echo, (1, 0, 2))
    reach = step_count * (taps.shape[-1] // 2)
    assert reach == own.shape[1]
    left, right = exchange(own, own, "sector")
    pieces = [left, own, right]
    result = None
    for step in range(step_count):
        angles = from_root(nav_angles, "sector", owner[step])
        last = step == step_count - 1
        result = compress_step(
            pieces, jnp.cos(angles), jnp.sin(angles), filters[step],
            jnp.float32 if last else jnp.bfloat16,
        )
        pieces = [result]
    energy = lax.psum(jnp.sum(result * result, axis=(0, 2)), "range")
    row_scale = lax.rsqrt(energy / (2.0 * RANGE) + 1e-05)
    scaled = (result * row_scale[None, :, None]).astype(jnp.bfloat16)
    return jnp.transpose(scaled, (1, 0, 2))


def solution(mesh):
    placed = (
        P("sector", None, "range"),
        P("sector", "range"),
        P(),
        P(None, "range", None, None),
        P("range"),
    )
    return jax.shard_map(
        on_device, mesh=mesh, in_specs=placed, out_specs=P("sector", None, "range"), check_vma=False
    )
```

```python
import functools

import jax
import jax.numpy as jnp
from jax import lax
from jax.experimental import pallas as pl
from jax.experimental.pallas import tpu as pltpu
from jax.sharding import PartitionSpec as P

RANGE = 8192


def from_root(value, axis, source):
    count = lax.axis_size(axis)
    kept = jnp.where(lax.axis_index(axis) == source, value, 0).astype(value.dtype)
    bit = 1
    while bit < count:
        pairs = [(i, i ^ bit) for i in range(count)]
        kept = kept + lax.ppermute(kept, axis, pairs)
        bit *= 2
    return kept


def exchange(low_rows, high_rows, axis):
    count = lax.axis_size(axis)
    forward = [(i, (i + 1) % count) for i in range(count)]
    backward = [((i + 1) % count, i) for i in range(count)]
    low = lax.ppermute(high_rows, axis, forward)
    high = lax.ppermute(low_rows, axis, backward)
    return low, high


def make_taps(taps, band):
    taps_count = taps.shape[-1]
    half_taps = taps_count // 2
    offsets = jnp.arange(taps_count, dtype=jnp.int32) - half_taps
    band_col = band[:, None]
    inside = (offsets[None, :] >= -band_col) & (offsets[None, :] < band_col)
    band_gain = jnp.sqrt(half_taps / band.astype(jnp.float32))
    weighted = (
        taps.astype(jnp.float32)
        * inside[None, :, None, :].astype(jnp.float32)
        * band_gain[None, :, None, None]
    )
    return weighted.astype(jnp.bfloat16)


def turn_rows(re, im, cosine, sine):
    period = cosine.shape[0]
    rows, width = re.shape
    re = re.astype(jnp.float32).reshape(rows // period, period, width)
    im = im.astype(jnp.float32).reshape(rows // period, period, width)
    real_part = re * cosine[None] - im * sine[None]
    imag_part = re * sine[None] + im * cosine[None]
    return (
        real_part.reshape(rows, width).astype(jnp.bfloat16),
        imag_part.reshape(rows, width).astype(jnp.bfloat16),
    )


def toeplitz_rows(weights, window):
    taps = weights.shape[-1]
    base = jnp.concatenate(
        [jnp.broadcast_to(weights, (taps, taps)), jnp.zeros((taps, window - taps), weights.dtype)],
        axis=1,
    )
    return pltpu.roll(base, 0, 1, stride=1, stride_axis=0)


def step_kernel(turn_flags, *refs):
    *pieces, cos_ref, sin_ref, f_ref, o_ref, re_s, im_s = refs
    offset = 0
    for piece, turn in zip(pieces, turn_flags):
        rows = piece.shape[1]
        if turn:
            re_t, im_t = turn_rows(piece[0], piece[1], cos_ref[...], sin_ref[...])
        else:
            re_t, im_t = piece[0], piece[1]
        re_s[offset : offset + rows] = re_t
        im_s[offset : offset + rows] = im_t
        offset += rows
    weights = f_ref[0]
    tile = weights.shape[-1]
    window = 2 * tile
    toep_real = toeplitz_rows(weights[0:1], window)
    toep_imag = toeplitz_rows(weights[1:2], window)
    from_real = jnp.concatenate([toep_real, toep_imag], axis=0).astype(jnp.bfloat16)
    from_imag = jnp.concatenate([-toep_imag, toep_real], axis=0).astype(jnp.bfloat16)
    for q in range(offset // tile - 1):
        start = q * tile
        acc = jnp.dot(from_real, re_s[start : start + window], preferred_element_type=jnp.float32)
        acc = acc + jnp.dot(
            from_imag, im_s[start : start + window], preferred_element_type=jnp.float32
        )
        o_ref[0, start : start + tile] = acc[:tile].astype(o_ref.dtype)
        o_ref[1, start : start + tile] = acc[tile:].astype(o_ref.dtype)


def compress_step(pieces, turn_flags, cosine, sine, weights, out_dtype):
    width = pieces[0].shape[2]
    rows = sum(piece.shape[1] for piece in pieces)
    blocks = weights.shape[0]
    bins = width // blocks
    period = cosine.shape[0]
    out_rows = rows - weights.shape[-1]
    return pl.pallas_call(
        functools.partial(step_kernel, tuple(turn_flags)),
        grid=(blocks,),
        in_specs=[pl.BlockSpec((2, piece.shape[1], bins), lambda b: (0, 0, b)) for piece in pieces]
        + [
            pl.BlockSpec((period, bins), lambda b: (0, b)),
            pl.BlockSpec((period, bins), lambda b: (0, b)),
            pl.BlockSpec((1,) + weights.shape[1:], lambda b: (b, 0, 0)),
        ],
        out_specs=pl.BlockSpec((2, out_rows, bins), lambda b: (0, 0, b)),
        out_shape=jax.ShapeDtypeStruct((2, out_rows, width), out_dtype),
        scratch_shapes=[
            pltpu.VMEM((rows, bins), jnp.bfloat16),
            pltpu.VMEM((rows, bins), jnp.bfloat16),
        ],
        compiler_params=pltpu.CompilerParams(dimension_semantics=("arbitrary",)),
    )(*pieces, cosine, sine, weights)


def on_device(echo, nav_angles, owner, taps, band):
    filters = make_taps(taps, band).astype(jnp.float32)
    step_count = taps.shape[0]
    halo = taps.shape[-1] // 2
    current = jnp.transpose(echo, (1, 0, 2))
    rows = current.shape[1]
    low, high = exchange(current[:, :halo], current[:, rows - halo :], "sector")
    turned_halo = True
    result = None
    for step in range(step_count):
        angles = from_root(nav_angles, "sector", owner[step])
        cosine = jnp.cos(angles)
        sine = jnp.sin(angles)
        if step > 0:
            low_re, low_im = turn_rows(current[0, :halo], current[1, :halo], cosine, sine)
            high_re, high_im = turn_rows(
                current[0, rows - halo :], current[1, rows - halo :], cosine, sine
            )
            low, high = exchange(
                jnp.stack([low_re, low_im]), jnp.stack([high_re, high_im]), "sector"
            )
            turned_halo = False
        last = step == step_count - 1
        result = compress_step(
            [low, current, high], (turned_halo, True, turned_halo), cosine, sine, filters[step],
            jnp.float32 if last else jnp.bfloat16,
        )
        current = result
    energy = lax.psum(jnp.sum(result * result, axis=(0, 2)), "range")
    row_scale = lax.rsqrt(energy / (2.0 * RANGE) + 1e-05)
    scaled = (result * row_scale[None, :, None]).astype(jnp.bfloat16)
    return jnp.transpose(scaled, (1, 0, 2))


def solution(mesh):
    placed = (
        P("sector", None, "range"),
        P("sector", "range"),
        P(),
        P(None, "range", None, None),
        P("range"),
    )
    return jax.shard_map(
        on_device, mesh=mesh, in_specs=placed, out_specs=P("sector", None, "range"), check_vma=False
    )
```

```python
import functools

import jax
import jax.numpy as jnp
from jax import lax
from jax.experimental import pallas as pl
from jax.experimental.pallas import tpu as pltpu
from jax.sharding import PartitionSpec as P

RANGE = 8192


def from_roots(value, axis, sources):
    count = lax.axis_size(axis)
    me = lax.axis_index(axis)
    kept = jnp.stack([jnp.where(me == source, value, 0).astype(value.dtype) for source in sources])
    flat = kept.reshape(count, -1)
    part = lax.all_to_all(flat, axis, 0, 0, tiled=True)
    mine = jnp.sum(part, axis=0, keepdims=True)
    full = lax.all_to_all(jnp.broadcast_to(mine, flat.shape), axis, 0, 0, tiled=True)
    return full.reshape(kept.shape)


def exchange(low_rows, high_rows, axis):
    count = lax.axis_size(axis)
    forward = [(i, (i + 1) % count) for i in range(count)]
    backward = [((i + 1) % count, i) for i in range(count)]
    low = lax.ppermute(high_rows, axis, forward)
    high = lax.ppermute(low_rows, axis, backward)
    return low, high


def make_taps(taps, band):
    taps_count = taps.shape[-1]
    half_taps = taps_count // 2
    offsets = jnp.arange(taps_count, dtype=jnp.int32) - half_taps
    band_col = band[:, None]
    inside = (offsets[None, :] >= -band_col) & (offsets[None, :] < band_col)
    band_gain = jnp.sqrt(half_taps / band.astype(jnp.float32))
    weighted = (
        taps.astype(jnp.float32)
        * inside[None, :, None, :].astype(jnp.float32)
        * band_gain[None, :, None, None]
    )
    return weighted.astype(jnp.bfloat16)


def turn_rows(re, im, cosine, sine):
    period = cosine.shape[0]
    rows, width = re.shape
    re = re.astype(jnp.float32).reshape(rows // period, period, width)
    im = im.astype(jnp.float32).reshape(rows // period, period, width)
    real_part = re * cosine[None] - im * sine[None]
    imag_part = re * sine[None] + im * cosine[None]
    return (
        real_part.reshape(rows, width).astype(jnp.bfloat16),
        imag_part.reshape(rows, width).astype(jnp.bfloat16),
    )


def toeplitz_rows(weights, window):
    taps = weights.shape[-1]
    base = jnp.concatenate(
        [jnp.broadcast_to(weights, (taps, taps)), jnp.zeros((taps, window - taps), weights.dtype)],
        axis=1,
    )
    return pltpu.roll(base, 0, 1, stride=1, stride_axis=0)


def step_kernel(x_ref, lo_ref, hi_ref, cos_ref, sin_ref, f_ref, o_ref, re_s, im_s):
    halo = lo_ref.shape[1]
    rows_in = x_ref.shape[1]
    re_t, im_t = turn_rows(x_ref[0], x_ref[1], cos_ref[...], sin_ref[...])
    re_s[0:halo] = lo_ref[0]
    im_s[0:halo] = lo_ref[1]
    re_s[halo : halo + rows_in] = re_t
    im_s[halo : halo + rows_in] = im_t
    re_s[halo + rows_in :] = hi_ref[0]
    im_s[halo + rows_in :] = hi_ref[1]
    weights = f_ref[0]
    tile = weights.shape[-1]
    window = 2 * tile
    toep_real = toeplitz_rows(weights[0:1], window)
    toep_imag = toeplitz_rows(weights[1:2], window)
    from_real = jnp.concatenate([toep_real, toep_imag], axis=0).astype(jnp.bfloat16)
    from_imag = jnp.concatenate([-toep_imag, toep_real], axis=0).astype(jnp.bfloat16)
    for q in range(rows_in // tile):
        start = q * tile
        acc = jnp.dot(from_real, re_s[start : start + window], preferred_element_type=jnp.float32)
        acc = acc + jnp.dot(
            from_imag, im_s[start : start + window], preferred_element_type=jnp.float32
        )
        o_ref[0, start : start + tile] = acc[:tile].astype(o_ref.dtype)
        o_ref[1, start : start + tile] = acc[tile:].astype(o_ref.dtype)


def compress_step(x, low, high, cosine, sine, weights, out_dtype):
    _, rows, width = x.shape
    blocks = weights.shape[0]
    bins = width // blocks
    halo = low.shape[1]
    period = cosine.shape[0]
    return pl.pallas_call(
        step_kernel,
        grid=(blocks,),
        in_specs=[
            pl.BlockSpec((2, rows, bins), lambda b: (0, 0, b)),
            pl.BlockSpec((2, halo, bins), lambda b: (0, 0, b)),
            pl.BlockSpec((2, halo, bins), lambda b: (0, 0, b)),
            pl.BlockSpec((period, bins), lambda b: (0, b)),
            pl.BlockSpec((period, bins), lambda b: (0, b)),
            pl.BlockSpec((1,) + weights.shape[1:], lambda b: (b, 0, 0)),
        ],
        out_specs=pl.BlockSpec((2, rows, bins), lambda b: (0, 0, b)),
        out_shape=jax.ShapeDtypeStruct(x.shape, out_dtype),
        scratch_shapes=[
            pltpu.VMEM((rows + 2 * halo, bins), jnp.bfloat16),
            pltpu.VMEM((rows + 2 * halo, bins), jnp.bfloat16),
        ],
        compiler_params=pltpu.CompilerParams(dimension_semantics=("arbitrary",)),
    )(x, low, high, cosine, sine, weights)


def on_device(echo, nav_angles, owner, taps, band):
    filters = make_taps(taps, band).astype(jnp.float32)
    step_count = taps.shape[0]
    halo = taps.shape[-1] // 2
    current = jnp.transpose(echo, (1, 0, 2))
    rows = current.shape[1]
    result = None
    all_angles = from_roots(nav_angles, "sector", [owner[step] for step in range(step_count)])
    for step in range(step_count):
        angles = all_angles[step]
        cosine = jnp.cos(angles)
        sine = jnp.sin(angles)
        low_re, low_im = turn_rows(current[0, :halo], current[1, :halo], cosine, sine)
        high_re, high_im = turn_rows(current[0, rows - halo :], current[1, rows - halo :], cosine, sine)
        low, high = exchange(
            jnp.stack([low_re, low_im]), jnp.stack([high_re, high_im]), "sector"
        )
        last = step == step_count - 1
        result = compress_step(
            current, low, high, cosine, sine, filters[step],
            jnp.float32 if last else jnp.bfloat16,
        )
        current = result
    energy = lax.psum(jnp.sum(result * result, axis=(0, 2)), "range")
    row_scale = lax.rsqrt(energy / (2.0 * RANGE) + 1e-05)
    scaled = (result * row_scale[None, :, None]).astype(jnp.bfloat16)
    return jnp.transpose(scaled, (1, 0, 2))


def solution(mesh):
    placed = (
        P("sector", None, "range"),
        P("sector", "range"),
        P(),
        P(None, "range", None, None),
        P("range"),
    )
    return jax.shard_map(
        on_device, mesh=mesh, in_specs=placed, out_specs=P("sector", None, "range"), check_vma=False
    )
```

```python
import functools

import jax
import jax.numpy as jnp
from jax import lax
from jax.experimental import pallas as pl
from jax.experimental.pallas import tpu as pltpu
from jax.sharding import PartitionSpec as P

RANGE = 8192


def from_roots(value, axis, sources, tied):
    count = lax.axis_size(axis)
    me = lax.axis_index(axis)
    kept = jnp.stack([jnp.where(me == source, value, 0).astype(value.dtype) for source in sources])
    flat = kept.reshape(count, -1)
    part = lax.all_to_all(flat, axis, 0, 0, tiled=True)
    mine = jnp.sum(part, axis=0, keepdims=True)
    mine, tied = lax.optimization_barrier((mine, tied))
    full = lax.all_to_all(jnp.broadcast_to(mine, flat.shape), axis, 0, 0, tiled=True)
    return full.reshape(kept.shape), tied


def exchange(low_rows, high_rows, axis):
    count = lax.axis_size(axis)
    forward = [(i, (i + 1) % count) for i in range(count)]
    backward = [((i + 1) % count, i) for i in range(count)]
    low = lax.ppermute(high_rows, axis, forward)
    high = lax.ppermute(low_rows, axis, backward)
    return low, high


def make_taps(taps, band):
    taps_count = taps.shape[-1]
    half_taps = taps_count // 2
    offsets = jnp.arange(taps_count, dtype=jnp.int32) - half_taps
    band_col = band[:, None]
    inside = (offsets[None, :] >= -band_col) & (offsets[None, :] < band_col)
    band_gain = jnp.sqrt(half_taps / band.astype(jnp.float32))
    weighted = (
        taps.astype(jnp.float32)
        * inside[None, :, None, :].astype(jnp.float32)
        * band_gain[None, :, None, None]
    )
    return weighted.astype(jnp.bfloat16)


def turn_rows(re, im, cosine, sine):
    period = cosine.shape[0]
    rows, width = re.shape
    re = re.astype(jnp.float32).reshape(rows // period, period, width)
    im = im.astype(jnp.float32).reshape(rows // period, period, width)
    real_part = re * cosine[None] - im * sine[None]
    imag_part = re * sine[None] + im * cosine[None]
    return (
        real_part.reshape(rows, width).astype(jnp.bfloat16),
        imag_part.reshape(rows, width).astype(jnp.bfloat16),
    )


def toeplitz_rows(weights, window):
    taps = weights.shape[-1]
    base = jnp.concatenate(
        [jnp.broadcast_to(weights, (taps, taps)), jnp.zeros((taps, window - taps), weights.dtype)],
        axis=1,
    )
    return pltpu.roll(base, 0, 1, stride=1, stride_axis=0)


def step_kernel(turn_flags, *refs):
    *pieces, cos_ref, sin_ref, f_ref, o_ref, re_s, im_s = refs
    offset = 0
    for piece, turn in zip(pieces, turn_flags):
        rows = piece.shape[1]
        if turn:
            re_t, im_t = turn_rows(piece[0], piece[1], cos_ref[...], sin_ref[...])
        else:
            re_t, im_t = piece[0], piece[1]
        re_s[offset : offset + rows] = re_t
        im_s[offset : offset + rows] = im_t
        offset += rows
    weights = f_ref[0]
    tile = weights.shape[-1]
    window = 2 * tile
    toep_real = toeplitz_rows(weights[0:1], window)
    toep_imag = toeplitz_rows(weights[1:2], window)
    from_real = jnp.concatenate([toep_real, toep_imag], axis=0).astype(jnp.bfloat16)
    from_imag = jnp.concatenate([-toep_imag, toep_real], axis=0).astype(jnp.bfloat16)
    for q in range(offset // tile - 1):
        start = q * tile
        acc = jnp.dot(from_real, re_s[start : start + window], preferred_element_type=jnp.float32)
        acc = acc + jnp.dot(
            from_imag, im_s[start : start + window], preferred_element_type=jnp.float32
        )
        o_ref[0, start : start + tile] = acc[:tile].astype(o_ref.dtype)
        o_ref[1, start : start + tile] = acc[tile:].astype(o_ref.dtype)


def compress_step(pieces, turn_flags, cosine, sine, weights, out_dtype):
    width = pieces[0].shape[2]
    rows = sum(piece.shape[1] for piece in pieces)
    blocks = weights.shape[0]
    bins = width // blocks
    period = cosine.shape[0]
    out_rows = rows - weights.shape[-1]
    return pl.pallas_call(
        functools.partial(step_kernel, tuple(turn_flags)),
        grid=(blocks,),
        in_specs=[pl.BlockSpec((2, piece.shape[1], bins), lambda b: (0, 0, b)) for piece in pieces]
        + [
            pl.BlockSpec((period, bins), lambda b: (0, b)),
            pl.BlockSpec((period, bins), lambda b: (0, b)),
            pl.BlockSpec((1,) + weights.shape[1:], lambda b: (b, 0, 0)),
        ],
        out_specs=pl.BlockSpec((2, out_rows, bins), lambda b: (0, 0, b)),
        out_shape=jax.ShapeDtypeStruct((2, out_rows, width), out_dtype),
        scratch_shapes=[
            pltpu.VMEM((rows, bins), jnp.bfloat16),
            pltpu.VMEM((rows, bins), jnp.bfloat16),
        ],
        compiler_params=pltpu.CompilerParams(dimension_semantics=("arbitrary",)),
    )(*pieces, cosine, sine, weights)


def on_device(echo, nav_angles, owner, taps, band):
    filters = make_taps(taps, band).astype(jnp.float32)
    step_count = taps.shape[0]
    halo = taps.shape[-1] // 2
    current = jnp.transpose(echo, (1, 0, 2))
    rows = current.shape[1]
    low, high = exchange(current[:, :halo], current[:, rows - halo :], "sector")
    all_angles, (low, high) = from_roots(
        nav_angles, "sector", [owner[step] for step in range(step_count)], (low, high)
    )
    turned_halo = True
    result = None
    for step in range(step_count):
        angles = all_angles[step]
        cosine = jnp.cos(angles)
        sine = jnp.sin(angles)
        if step > 0:
            low_re, low_im = turn_rows(current[0, :halo], current[1, :halo], cosine, sine)
            high_re, high_im = turn_rows(
                current[0, rows - halo :], current[1, rows - halo :], cosine, sine
            )
            low, high = exchange(
                jnp.stack([low_re, low_im]), jnp.stack([high_re, high_im]), "sector"
            )
            turned_halo = False
        last = step == step_count - 1
        result = compress_step(
            [low, current, high], (turned_halo, True, turned_halo), cosine, sine, filters[step],
            jnp.float32 if last else jnp.bfloat16,
        )
        current = result
    energy = lax.psum(jnp.sum(result * result, axis=(0, 2)), "range")
    row_scale = lax.rsqrt(energy / (2.0 * RANGE) + 1e-05)
    scaled = (result * row_scale[None, :, None]).astype(jnp.bfloat16)
    return jnp.transpose(scaled, (1, 0, 2))


def solution(mesh):
    placed = (
        P("sector", None, "range"),
        P("sector", "range"),
        P(),
        P(None, "range", None, None),
        P("range"),
    )
    return jax.shard_map(
        on_device, mesh=mesh, in_specs=placed, out_specs=P("sector", None, "range"), check_vma=False
    )
```

```python
import functools

import jax
import jax.numpy as jnp
from jax import lax
from jax.experimental import pallas as pl
from jax.experimental.pallas import tpu as pltpu
from jax.sharding import PartitionSpec as P

RANGE = 8192


def from_roots(value, axis, sources, tied):
    count = lax.axis_size(axis)
    me = lax.axis_index(axis)
    kept = jnp.stack([jnp.where(me == source, value, 0) for source in sources]).astype(jnp.bfloat16)
    flat = kept.reshape(count, -1)
    part = lax.all_to_all(flat, axis, 0, 0, tiled=True)
    mine = jnp.sum(part, axis=0, keepdims=True)
    mine, tied = lax.optimization_barrier((mine, tied))
    full = lax.all_to_all(jnp.broadcast_to(mine, flat.shape), axis, 0, 0, tiled=True)
    return full.reshape(kept.shape).astype(value.dtype), tied


def exchange(low_rows, high_rows, axis):
    count = lax.axis_size(axis)
    forward = [(i, (i + 1) % count) for i in range(count)]
    backward = [((i + 1) % count, i) for i in range(count)]
    low = lax.ppermute(high_rows, axis, forward)
    high = lax.ppermute(low_rows, axis, backward)
    return low, high


def make_taps(taps, band):
    taps_count = taps.shape[-1]
    half_taps = taps_count // 2
    offsets = jnp.arange(taps_count, dtype=jnp.int32) - half_taps
    band_col = band[:, None]
    inside = (offsets[None, :] >= -band_col) & (offsets[None, :] < band_col)
    band_gain = jnp.sqrt(half_taps / band.astype(jnp.float32))
    weighted = (
        taps.astype(jnp.float32)
        * inside[None, :, None, :].astype(jnp.float32)
        * band_gain[None, :, None, None]
    )
    return weighted.astype(jnp.bfloat16)


def turn_rows(re, im, cosine, sine):
    period = cosine.shape[0]
    rows, width = re.shape
    re = re.astype(jnp.float32).reshape(rows // period, period, width)
    im = im.astype(jnp.float32).reshape(rows // period, period, width)
    real_part = re * cosine[None] - im * sine[None]
    imag_part = re * sine[None] + im * cosine[None]
    return (
        real_part.reshape(rows, width).astype(jnp.bfloat16),
        imag_part.reshape(rows, width).astype(jnp.bfloat16),
    )


def toeplitz_rows(weights, window):
    taps = weights.shape[-1]
    base = jnp.concatenate(
        [jnp.broadcast_to(weights, (taps, taps)), jnp.zeros((taps, window - taps), weights.dtype)],
        axis=1,
    )
    return pltpu.roll(base, 0, 1, stride=1, stride_axis=0)


def step_kernel(turn_flags, *refs):
    *pieces, cos_ref, sin_ref, f_ref, o_ref, re_s, im_s = refs
    offset = 0
    for piece, turn in zip(pieces, turn_flags):
        rows = piece.shape[1]
        if turn:
            re_t, im_t = turn_rows(piece[0], piece[1], cos_ref[...], sin_ref[...])
        else:
            re_t, im_t = piece[0], piece[1]
        re_s[offset : offset + rows] = re_t
        im_s[offset : offset + rows] = im_t
        offset += rows
    weights = f_ref[0]
    tile = weights.shape[-1]
    window = 2 * tile
    toep_real = toeplitz_rows(weights[0:1], window)
    toep_imag = toeplitz_rows(weights[1:2], window)
    from_real = jnp.concatenate([toep_real, toep_imag], axis=0).astype(jnp.bfloat16)
    from_imag = jnp.concatenate([-toep_imag, toep_real], axis=0).astype(jnp.bfloat16)
    for q in range(offset // tile - 1):
        start = q * tile
        acc = jnp.dot(from_real, re_s[start : start + window], preferred_element_type=jnp.float32)
        acc = acc + jnp.dot(
            from_imag, im_s[start : start + window], preferred_element_type=jnp.float32
        )
        o_ref[0, start : start + tile] = acc[:tile].astype(o_ref.dtype)
        o_ref[1, start : start + tile] = acc[tile:].astype(o_ref.dtype)


def compress_step(pieces, turn_flags, cosine, sine, weights, out_dtype):
    width = pieces[0].shape[2]
    rows = sum(piece.shape[1] for piece in pieces)
    blocks = weights.shape[0]
    bins = width // blocks
    period = cosine.shape[0]
    out_rows = rows - weights.shape[-1]
    return pl.pallas_call(
        functools.partial(step_kernel, tuple(turn_flags)),
        grid=(blocks,),
        in_specs=[pl.BlockSpec((2, piece.shape[1], bins), lambda b: (0, 0, b)) for piece in pieces]
        + [
            pl.BlockSpec((period, bins), lambda b: (0, b)),
            pl.BlockSpec((period, bins), lambda b: (0, b)),
            pl.BlockSpec((1,) + weights.shape[1:], lambda b: (b, 0, 0)),
        ],
        out_specs=pl.BlockSpec((2, out_rows, bins), lambda b: (0, 0, b)),
        out_shape=jax.ShapeDtypeStruct((2, out_rows, width), out_dtype),
        scratch_shapes=[
            pltpu.VMEM((rows, bins), jnp.bfloat16),
            pltpu.VMEM((rows, bins), jnp.bfloat16),
        ],
        compiler_params=pltpu.CompilerParams(dimension_semantics=("arbitrary",)),
    )(*pieces, cosine, sine, weights)


def on_device(echo, nav_angles, owner, taps, band):
    filters = make_taps(taps, band).astype(jnp.float32)
    step_count = taps.shape[0]
    halo = taps.shape[-1] // 2
    current = jnp.transpose(echo, (1, 0, 2))
    rows = current.shape[1]
    low, high = exchange(current[:, :halo], current[:, rows - halo :], "sector")
    all_angles, (low, high) = from_roots(
        nav_angles, "sector", [owner[step] for step in range(step_count)], (low, high)
    )
    turned_halo = True
    result = None
    for step in range(step_count):
        angles = all_angles[step]
        cosine = jnp.cos(angles)
        sine = jnp.sin(angles)
        if step > 0:
            low_re, low_im = turn_rows(current[0, :halo], current[1, :halo], cosine, sine)
            high_re, high_im = turn_rows(
                current[0, rows - halo :], current[1, rows - halo :], cosine, sine
            )
            low, high = exchange(
                jnp.stack([low_re, low_im]), jnp.stack([high_re, high_im]), "sector"
            )
            turned_halo = False
        last = step == step_count - 1
        result = compress_step(
            [low, current, high], (turned_halo, True, turned_halo), cosine, sine, filters[step],
            jnp.float32 if last else jnp.bfloat16,
        )
        current = result
    energy = lax.psum(jnp.sum(result * result, axis=(0, 2)), "range")
    row_scale = lax.rsqrt(energy / (2.0 * RANGE) + 1e-05)
    scaled = (result * row_scale[None, :, None]).astype(jnp.bfloat16)
    return jnp.transpose(scaled, (1, 0, 2))


def solution(mesh):
    placed = (
        P("sector", None, "range"),
        P("sector", "range"),
        P(),
        P(None, "range", None, None),
        P("range"),
    )
    return jax.shard_map(
        on_device, mesh=mesh, in_specs=placed, out_specs=P("sector", None, "range"), check_vma=False
    )
```

```python
import functools

import jax
import jax.numpy as jnp
from jax import lax
from jax.experimental import pallas as pl
from jax.experimental.pallas import tpu as pltpu
from jax.sharding import PartitionSpec as P

RANGE = 8192


def from_roots(value, axis, sources, tied):
    count = lax.axis_size(axis)
    me = lax.axis_index(axis)
    kept = jnp.stack([jnp.where(me == source, value, 0) for source in sources]).astype(jnp.bfloat16)
    flat = kept.reshape(count, -1)
    part = lax.all_to_all(flat, axis, 0, 0, tiled=True)
    mine = jnp.sum(part, axis=0, keepdims=True)
    full = lax.all_to_all(jnp.broadcast_to(mine, flat.shape), axis, 0, 0, tiled=True)
    full, tied = lax.optimization_barrier((full, tied))
    return full.reshape(kept.shape).astype(value.dtype), tied


def exchange(low_rows, high_rows, axis):
    count = lax.axis_size(axis)
    forward = [(i, (i + 1) % count) for i in range(count)]
    backward = [((i + 1) % count, i) for i in range(count)]
    low = lax.ppermute(high_rows, axis, forward)
    high = lax.ppermute(low_rows, axis, backward)
    return low, high


def make_taps(taps, band):
    taps_count = taps.shape[-1]
    half_taps = taps_count // 2
    offsets = jnp.arange(taps_count, dtype=jnp.int32) - half_taps
    band_col = band[:, None]
    inside = (offsets[None, :] >= -band_col) & (offsets[None, :] < band_col)
    band_gain = jnp.sqrt(half_taps / band.astype(jnp.float32))
    weighted = (
        taps.astype(jnp.float32)
        * inside[None, :, None, :].astype(jnp.float32)
        * band_gain[None, :, None, None]
    )
    return weighted.astype(jnp.bfloat16)


def turn_rows(re, im, cosine, sine):
    period = cosine.shape[0]
    rows, width = re.shape
    re = re.astype(jnp.float32).reshape(rows // period, period, width)
    im = im.astype(jnp.float32).reshape(rows // period, period, width)
    real_part = re * cosine[None] - im * sine[None]
    imag_part = re * sine[None] + im * cosine[None]
    return (
        real_part.reshape(rows, width).astype(jnp.bfloat16),
        imag_part.reshape(rows, width).astype(jnp.bfloat16),
    )


def toeplitz_rows(weights, window):
    taps = weights.shape[-1]
    base = jnp.concatenate(
        [jnp.broadcast_to(weights, (taps, taps)), jnp.zeros((taps, window - taps), weights.dtype)],
        axis=1,
    )
    return pltpu.roll(base, 0, 1, stride=1, stride_axis=0)


def step_kernel(turn_flags, *refs):
    *pieces, cos_ref, sin_ref, f_ref, o_ref, re_s, im_s = refs
    offset = 0
    for piece, turn in zip(pieces, turn_flags):
        rows = piece.shape[1]
        if turn:
            re_t, im_t = turn_rows(piece[0], piece[1], cos_ref[...], sin_ref[...])
        else:
            re_t, im_t = piece[0], piece[1]
        re_s[offset : offset + rows] = re_t
        im_s[offset : offset + rows] = im_t
        offset += rows
    weights = f_ref[0]
    tile = weights.shape[-1]
    window = 2 * tile
    toep_real = toeplitz_rows(weights[0:1], window)
    toep_imag = toeplitz_rows(weights[1:2], window)
    from_real = jnp.concatenate([toep_real, toep_imag], axis=0).astype(jnp.bfloat16)
    from_imag = jnp.concatenate([-toep_imag, toep_real], axis=0).astype(jnp.bfloat16)
    for q in range(offset // tile - 1):
        start = q * tile
        acc = jnp.dot(from_real, re_s[start : start + window], preferred_element_type=jnp.float32)
        acc = acc + jnp.dot(
            from_imag, im_s[start : start + window], preferred_element_type=jnp.float32
        )
        o_ref[0, start : start + tile] = acc[:tile].astype(o_ref.dtype)
        o_ref[1, start : start + tile] = acc[tile:].astype(o_ref.dtype)


def compress_step(pieces, turn_flags, cosine, sine, weights, out_dtype):
    width = pieces[0].shape[2]
    rows = sum(piece.shape[1] for piece in pieces)
    blocks = weights.shape[0]
    bins = width // blocks
    period = cosine.shape[0]
    out_rows = rows - weights.shape[-1]
    return pl.pallas_call(
        functools.partial(step_kernel, tuple(turn_flags)),
        grid=(blocks,),
        in_specs=[pl.BlockSpec((2, piece.shape[1], bins), lambda b: (0, 0, b)) for piece in pieces]
        + [
            pl.BlockSpec((period, bins), lambda b: (0, b)),
            pl.BlockSpec((period, bins), lambda b: (0, b)),
            pl.BlockSpec((1,) + weights.shape[1:], lambda b: (b, 0, 0)),
        ],
        out_specs=pl.BlockSpec((2, out_rows, bins), lambda b: (0, 0, b)),
        out_shape=jax.ShapeDtypeStruct((2, out_rows, width), out_dtype),
        scratch_shapes=[
            pltpu.VMEM((rows, bins), jnp.bfloat16),
            pltpu.VMEM((rows, bins), jnp.bfloat16),
        ],
        compiler_params=pltpu.CompilerParams(dimension_semantics=("arbitrary",)),
    )(*pieces, cosine, sine, weights)


def on_device(echo, nav_angles, owner, taps, band):
    filters = make_taps(taps, band).astype(jnp.float32)
    step_count = taps.shape[0]
    own = jnp.transpose(echo, (1, 0, 2))
    reach = step_count * (taps.shape[-1] // 2)
    assert reach == own.shape[1]
    left, right = exchange(own, own, "sector")
    all_angles, (left, right) = from_roots(
        nav_angles, "sector", [owner[step] for step in range(step_count)], (left, right)
    )
    pieces = [left, own, right]
    result = None
    for step in range(step_count):
        angles = all_angles[step]
        last = step == step_count - 1
        result = compress_step(
            pieces, (True,) * len(pieces), jnp.cos(angles), jnp.sin(angles), filters[step],
            jnp.float32 if last else jnp.bfloat16,
        )
        pieces = [result]
    energy = lax.psum(jnp.sum(result * result, axis=(0, 2)), "range")
    row_scale = lax.rsqrt(energy / (2.0 * RANGE) + 1e-05)
    scaled = (result * row_scale[None, :, None]).astype(jnp.bfloat16)
    return jnp.transpose(scaled, (1, 0, 2))


def solution(mesh):
    placed = (
        P("sector", None, "range"),
        P("sector", "range"),
        P(),
        P(None, "range", None, None),
        P("range"),
    )
    return jax.shard_map(
        on_device, mesh=mesh, in_specs=placed, out_specs=P("sector", None, "range"), check_vma=False
    )
```

```python
import functools

import jax
import jax.numpy as jnp
from jax import lax
from jax.experimental import pallas as pl
from jax.experimental.pallas import tpu as pltpu
from jax.sharding import PartitionSpec as P

RANGE = 8192


def from_roots(value, axis, sources, tied):
    count = lax.axis_size(axis)
    me = lax.axis_index(axis)
    kept = jnp.stack([jnp.where(me == source, value, 0) for source in sources]).astype(jnp.bfloat16)
    flat = kept.reshape(count, -1)
    part = lax.all_to_all(flat, axis, 0, 0, tiled=True)
    mine = jnp.sum(part, axis=0, keepdims=True)
    full = lax.all_to_all(jnp.broadcast_to(mine, flat.shape), axis, 0, 0, tiled=True)
    full, tied = lax.optimization_barrier((full, tied))
    return full.reshape(kept.shape).astype(value.dtype), tied


def exchange(low_rows, high_rows, axis):
    count = lax.axis_size(axis)
    forward = [(i, (i + 1) % count) for i in range(count)]
    backward = [((i + 1) % count, i) for i in range(count)]
    low = lax.ppermute(high_rows, axis, forward)
    high = lax.ppermute(low_rows, axis, backward)
    return low, high


def make_taps(taps, band):
    taps_count = taps.shape[-1]
    half_taps = taps_count // 2
    offsets = jnp.arange(taps_count, dtype=jnp.int32) - half_taps
    band_col = band[:, None]
    inside = (offsets[None, :] >= -band_col) & (offsets[None, :] < band_col)
    band_gain = jnp.sqrt(half_taps / band.astype(jnp.float32))
    weighted = (
        taps.astype(jnp.float32)
        * inside[None, :, None, :].astype(jnp.float32)
        * band_gain[None, :, None, None]
    )
    return weighted.astype(jnp.bfloat16)


def turn_rows(re, im, cosine, sine):
    period = cosine.shape[0]
    rows, width = re.shape
    re = re.astype(jnp.float32).reshape(rows // period, period, width)
    im = im.astype(jnp.float32).reshape(rows // period, period, width)
    real_part = re * cosine[None] - im * sine[None]
    imag_part = re * sine[None] + im * cosine[None]
    return (
        real_part.reshape(rows, width).astype(jnp.bfloat16),
        imag_part.reshape(rows, width).astype(jnp.bfloat16),
    )


def toeplitz_rows(weights, window):
    taps = weights.shape[-1]
    base = jnp.concatenate(
        [jnp.broadcast_to(weights, (taps, taps)), jnp.zeros((taps, window - taps), weights.dtype)],
        axis=1,
    )
    return pltpu.roll(base, 0, 1, stride=1, stride_axis=0)


def fused_kernel(left_ref, own_ref, right_ref, cos_ref, sin_ref, f_ref, o_ref, e_ref, re_s, im_s):
    steps = cos_ref.shape[0]
    offset = 0
    for piece in (left_ref, own_ref, right_ref):
        rows = piece.shape[1]
        re_t, im_t = turn_rows(piece[0], piece[1], cos_ref[0], sin_ref[0])
        re_s[offset : offset + rows] = re_t
        im_s[offset : offset + rows] = im_t
        offset += rows

    @pl.when(pl.program_id(0) == 0)
    def _():
        e_ref[...] = jnp.zeros_like(e_ref)

    weights = f_ref[0]
    tile = weights.shape[-1]
    window = 2 * tile
    lanes = e_ref.shape[-1]
    rows_in = offset
    for step in range(steps):
        toep_real = toeplitz_rows(weights[step, 0:1], window)
        toep_imag = toeplitz_rows(weights[step, 1:2], window)
        from_real = jnp.concatenate([toep_real, toep_imag], axis=0).astype(jnp.bfloat16)
        from_imag = jnp.concatenate([-toep_imag, toep_real], axis=0).astype(jnp.bfloat16)
        for q in range(rows_in // tile - 1):
            start = q * tile
            acc = jnp.dot(
                from_real, re_s[start : start + window], preferred_element_type=jnp.float32
            )
            acc = acc + jnp.dot(
                from_imag, im_s[start : start + window], preferred_element_type=jnp.float32
            )
            real_part = acc[:tile]
            imag_part = acc[tile:]
            if step < steps - 1:
                re_t, im_t = turn_rows(
                    real_part.astype(jnp.bfloat16), imag_part.astype(jnp.bfloat16),
                    cos_ref[step + 1], sin_ref[step + 1],
                )
                re_s[start : start + tile] = re_t
                im_s[start : start + tile] = im_t
            else:
                o_ref[0, start : start + tile] = real_part
                o_ref[1, start : start + tile] = imag_part
                power = real_part * real_part + imag_part * imag_part
                folded = power[:, :lanes]
                for k in range(1, power.shape[1] // lanes):
                    folded = folded + power[:, k * lanes : (k + 1) * lanes]
                e_ref[start : start + tile] += folded
        rows_in -= tile


def compress_all(pieces, cosine, sine, weights):
    width = pieces[0].shape[2]
    rows = sum(piece.shape[1] for piece in pieces)
    blocks = weights.shape[0]
    bins = width // blocks
    steps = cosine.shape[0]
    period = cosine.shape[1]
    out_rows = rows - steps * weights.shape[-1]
    lanes = 128
    return pl.pallas_call(
        fused_kernel,
        grid=(blocks,),
        in_specs=[pl.BlockSpec((2, piece.shape[1], bins), lambda b: (0, 0, b)) for piece in pieces]
        + [
            pl.BlockSpec((steps, period, bins), lambda b: (0, 0, b)),
            pl.BlockSpec((steps, period, bins), lambda b: (0, 0, b)),
            pl.BlockSpec((1,) + weights.shape[1:], lambda b: (b, 0, 0, 0)),
        ],
        out_specs=[
            pl.BlockSpec((2, out_rows, bins), lambda b: (0, 0, b)),
            pl.BlockSpec((out_rows, lanes), lambda b: (0, 0)),
        ],
        out_shape=[
            jax.ShapeDtypeStruct((2, out_rows, width), jnp.float32),
            jax.ShapeDtypeStruct((out_rows, lanes), jnp.float32),
        ],
        scratch_shapes=[
            pltpu.VMEM((rows, bins), jnp.bfloat16),
            pltpu.VMEM((rows, bins), jnp.bfloat16),
        ],
        compiler_params=pltpu.CompilerParams(dimension_semantics=("arbitrary",)),
    )(*pieces, cosine, sine, weights)


def on_device(echo, nav_angles, owner, taps, band):
    filters = jnp.transpose(make_taps(taps, band).astype(jnp.float32), (1, 0, 2, 3))
    step_count = taps.shape[0]
    own = jnp.transpose(echo, (1, 0, 2))
    reach = step_count * (taps.shape[-1] // 2)
    assert reach == own.shape[1]
    left, right = exchange(own, own, "sector")
    all_angles, (left, right) = from_roots(
        nav_angles, "sector", [owner[step] for step in range(step_count)], (left, right)
    )
    result, partial = compress_all(
        [left, own, right], jnp.cos(all_angles), jnp.sin(all_angles), filters
    )
    energy = lax.psum(jnp.sum(partial, axis=1), "range")
    row_scale = lax.rsqrt(energy / (2.0 * RANGE) + 1e-05)
    scaled = (result * row_scale[None, :, None]).astype(jnp.bfloat16)
    return jnp.transpose(scaled, (1, 0, 2))


def solution(mesh):
    placed = (
        P("sector", None, "range"),
        P("sector", "range"),
        P(),
        P(None, "range", None, None),
        P("range"),
    )
    return jax.shard_map(
        on_device, mesh=mesh, in_specs=placed, out_specs=P("sector", None, "range"), check_vma=False
    )
```

```python
import functools

import jax
import jax.numpy as jnp
from jax import lax
from jax.experimental import pallas as pl
from jax.experimental.pallas import tpu as pltpu
from jax.sharding import PartitionSpec as P

RANGE = 8192


def from_roots(value, axis, sources, tied):
    count = lax.axis_size(axis)
    me = lax.axis_index(axis)
    kept = jnp.stack([jnp.where(me == source, value, 0) for source in sources]).astype(jnp.bfloat16)
    flat = kept.reshape(count, -1)
    part = lax.all_to_all(flat, axis, 0, 0, tiled=True)
    mine = jnp.sum(part, axis=0, keepdims=True)
    full = lax.all_to_all(jnp.broadcast_to(mine, flat.shape), axis, 0, 0, tiled=True)
    full, tied = lax.optimization_barrier((full, tied))
    return full.reshape(kept.shape).astype(value.dtype), tied


def exchange(low_rows, high_rows, axis):
    count = lax.axis_size(axis)
    forward = [(i, (i + 1) % count) for i in range(count)]
    backward = [((i + 1) % count, i) for i in range(count)]
    low = lax.ppermute(high_rows, axis, forward)
    high = lax.ppermute(low_rows, axis, backward)
    return low, high


def make_taps(taps, band):
    taps_count = taps.shape[-1]
    half_taps = taps_count // 2
    offsets = jnp.arange(taps_count, dtype=jnp.int32) - half_taps
    band_col = band[:, None]
    inside = (offsets[None, :] >= -band_col) & (offsets[None, :] < band_col)
    band_gain = jnp.sqrt(half_taps / band.astype(jnp.float32))
    weighted = (
        taps.astype(jnp.float32)
        * inside[None, :, None, :].astype(jnp.float32)
        * band_gain[None, :, None, None]
    )
    return weighted.astype(jnp.bfloat16)


def turn_rows(re, im, cosine, sine):
    period = cosine.shape[0]
    rows, width = re.shape
    re = re.astype(jnp.float32).reshape(rows // period, period, width)
    im = im.astype(jnp.float32).reshape(rows // period, period, width)
    real_part = re * cosine[None] - im * sine[None]
    imag_part = re * sine[None] + im * cosine[None]
    return (
        real_part.reshape(rows, width).astype(jnp.bfloat16),
        imag_part.reshape(rows, width).astype(jnp.bfloat16),
    )


def toeplitz_rows(weights, window):
    taps = weights.shape[-1]
    base = jnp.concatenate(
        [jnp.broadcast_to(weights, (taps, taps)), jnp.zeros((taps, window - taps), weights.dtype)],
        axis=1,
    )
    return pltpu.roll(base, 0, 1, stride=1, stride_axis=0)


def fused_kernel(left_ref, own_ref, right_ref, a_ref, f_ref, o_ref, e_ref, re_s, im_s):
    angles = a_ref[...]
    cos_all = jnp.cos(angles)
    sin_all = jnp.sin(angles)
    steps = angles.shape[0]
    offset = 0
    for piece in (left_ref, own_ref, right_ref):
        rows = piece.shape[1]
        re_t, im_t = turn_rows(piece[0], piece[1], cos_all[0], sin_all[0])
        re_s[offset : offset + rows] = re_t
        im_s[offset : offset + rows] = im_t
        offset += rows

    @pl.when(pl.program_id(0) == 0)
    def _():
        e_ref[...] = jnp.zeros_like(e_ref)

    weights = f_ref[0]
    tile = weights.shape[-1]
    window = 2 * tile
    lanes = e_ref.shape[-1]
    rows_in = offset
    for step in range(steps):
        toep_real = toeplitz_rows(weights[step, 0:1], window)
        toep_imag = toeplitz_rows(weights[step, 1:2], window)
        from_real = jnp.concatenate([toep_real, toep_imag], axis=0).astype(jnp.bfloat16)
        from_imag = jnp.concatenate([-toep_imag, toep_real], axis=0).astype(jnp.bfloat16)
        for q in range(rows_in // tile - 1):
            start = q * tile
            acc = jnp.dot(
                from_real, re_s[start : start + window], preferred_element_type=jnp.float32
            )
            acc = acc + jnp.dot(
                from_imag, im_s[start : start + window], preferred_element_type=jnp.float32
            )
            real_part = acc[:tile]
            imag_part = acc[tile:]
            if step < steps - 1:
                re_t, im_t = turn_rows(
                    real_part.astype(jnp.bfloat16), imag_part.astype(jnp.bfloat16),
                    cos_all[step + 1], sin_all[step + 1],
                )
                re_s[start : start + tile] = re_t
                im_s[start : start + tile] = im_t
            else:
                o_ref[0, start : start + tile] = real_part
                o_ref[1, start : start + tile] = imag_part
                power = real_part * real_part + imag_part * imag_part
                folded = power[:, :lanes]
                for k in range(1, power.shape[1] // lanes):
                    folded = folded + power[:, k * lanes : (k + 1) * lanes]
                e_ref[start : start + tile] += folded
        rows_in -= tile


def compress_all(pieces, angles, weights):
    width = pieces[0].shape[2]
    rows = sum(piece.shape[1] for piece in pieces)
    blocks = weights.shape[0]
    bins = width // blocks
    steps = angles.shape[0]
    period = angles.shape[1]
    out_rows = rows - steps * weights.shape[-1]
    lanes = 128
    return pl.pallas_call(
        fused_kernel,
        grid=(blocks,),
        in_specs=[pl.BlockSpec((2, piece.shape[1], bins), lambda b: (0, 0, b)) for piece in pieces]
        + [
            pl.BlockSpec((steps, period, bins), lambda b: (0, 0, b)),
            pl.BlockSpec((1,) + weights.shape[1:], lambda b: (b, 0, 0, 0)),
        ],
        out_specs=[
            pl.BlockSpec((2, out_rows, bins), lambda b: (0, 0, b)),
            pl.BlockSpec((out_rows, lanes), lambda b: (0, 0)),
        ],
        out_shape=[
            jax.ShapeDtypeStruct((2, out_rows, width), jnp.float32),
            jax.ShapeDtypeStruct((out_rows, lanes), jnp.float32),
        ],
        scratch_shapes=[
            pltpu.VMEM((rows, bins), jnp.bfloat16),
            pltpu.VMEM((rows, bins), jnp.bfloat16),
        ],
        compiler_params=pltpu.CompilerParams(dimension_semantics=("arbitrary",)),
    )(*pieces, angles, weights)


def on_device(echo, nav_angles, owner, taps, band):
    filters = jnp.transpose(make_taps(taps, band).astype(jnp.float32), (1, 0, 2, 3))
    step_count = taps.shape[0]
    own = jnp.transpose(echo, (1, 0, 2))
    reach = step_count * (taps.shape[-1] // 2)
    assert reach == own.shape[1]
    left, right = exchange(own, own, "sector")
    all_angles, (left, right) = from_roots(
        nav_angles, "sector", [owner[step] for step in range(step_count)], (left, right)
    )
    result, partial = compress_all([left, own, right], all_angles, filters)
    energy = lax.psum(jnp.sum(partial, axis=1), "range")
    row_scale = lax.rsqrt(energy / (2.0 * RANGE) + 1e-05)
    scaled = (result * row_scale[None, :, None]).astype(jnp.bfloat16)
    return jnp.transpose(scaled, (1, 0, 2))


def solution(mesh):
    placed = (
        P("sector", None, "range"),
        P("sector", "range"),
        P(),
        P(None, "range", None, None),
        P("range"),
    )
    return jax.shard_map(
        on_device, mesh=mesh, in_specs=placed, out_specs=P("sector", None, "range"), check_vma=False
    )
```

```python
import functools

import jax
import jax.numpy as jnp
from jax import lax
from jax.experimental import pallas as pl
from jax.experimental.pallas import tpu as pltpu
from jax.sharding import PartitionSpec as P

RANGE = 8192


def from_roots(value, axis, sources, tied):
    count = lax.axis_size(axis)
    me = lax.axis_index(axis)
    kept = jnp.stack([jnp.where(me == source, value, 0) for source in sources]).astype(jnp.bfloat16)
    flat = kept.reshape(count, -1)
    part = lax.all_to_all(flat, axis, 0, 0, tiled=True)
    mine = jnp.sum(part, axis=0, keepdims=True)
    mine, tied = lax.optimization_barrier((mine, tied))
    return mine, tied, (flat.shape, kept.shape, value.dtype)


def gather_roots(mine, axis, shapes):
    flat_shape, kept_shape, dtype = shapes
    full = lax.all_to_all(jnp.broadcast_to(mine, flat_shape), axis, 0, 0, tiled=True)
    return full.reshape(kept_shape).astype(dtype)


def exchange(low_rows, high_rows, axis):
    count = lax.axis_size(axis)
    forward = [(i, (i + 1) % count) for i in range(count)]
    backward = [((i + 1) % count, i) for i in range(count)]
    low = lax.ppermute(high_rows, axis, forward)
    high = lax.ppermute(low_rows, axis, backward)
    return low, high


def make_taps(taps, band):
    taps_count = taps.shape[-1]
    half_taps = taps_count // 2
    offsets = jnp.arange(taps_count, dtype=jnp.int32) - half_taps
    band_col = band[:, None]
    inside = (offsets[None, :] >= -band_col) & (offsets[None, :] < band_col)
    band_gain = jnp.sqrt(half_taps / band.astype(jnp.float32))
    weighted = (
        taps.astype(jnp.float32)
        * inside[None, :, None, :].astype(jnp.float32)
        * band_gain[None, :, None, None]
    )
    return weighted.astype(jnp.bfloat16)


def turn_rows(re, im, cosine, sine):
    period = cosine.shape[0]
    rows, width = re.shape
    re = re.astype(jnp.float32).reshape(rows // period, period, width)
    im = im.astype(jnp.float32).reshape(rows // period, period, width)
    real_part = re * cosine[None] - im * sine[None]
    imag_part = re * sine[None] + im * cosine[None]
    return (
        real_part.reshape(rows, width).astype(jnp.bfloat16),
        imag_part.reshape(rows, width).astype(jnp.bfloat16),
    )


def toeplitz_rows(weights, window):
    taps = weights.shape[-1]
    base = jnp.concatenate(
        [jnp.broadcast_to(weights, (taps, taps)), jnp.zeros((taps, window - taps), weights.dtype)],
        axis=1,
    )
    return pltpu.roll(base, 0, 1, stride=1, stride_axis=0)


def fused_kernel(left_ref, own_ref, right_ref, a_ref, f_ref, o_ref, e_ref, re_s, im_s):
    angles = a_ref[...]
    cos_all = jnp.cos(angles)
    sin_all = jnp.sin(angles)
    steps = angles.shape[0]
    offset = 0
    for piece in (left_ref, own_ref, right_ref):
        rows = piece.shape[1]
        re_t, im_t = turn_rows(piece[0], piece[1], cos_all[0], sin_all[0])
        re_s[offset : offset + rows] = re_t
        im_s[offset : offset + rows] = im_t
        offset += rows

    @pl.when(pl.program_id(0) == 0)
    def _():
        e_ref[...] = jnp.zeros_like(e_ref)

    weights = f_ref[0]
    tile = weights.shape[-1]
    window = 2 * tile
    lanes = e_ref.shape[-1]
    rows_in = offset
    for step in range(steps):
        toep_real = toeplitz_rows(weights[step, 0:1], window)
        toep_imag = toeplitz_rows(weights[step, 1:2], window)
        from_real = jnp.concatenate([toep_real, toep_imag], axis=0).astype(jnp.bfloat16)
        from_imag = jnp.concatenate([-toep_imag, toep_real], axis=0).astype(jnp.bfloat16)
        for q in range(rows_in // tile - 1):
            start = q * tile
            acc = jnp.dot(
                from_real, re_s[start : start + window], preferred_element_type=jnp.float32
            )
            acc = acc + jnp.dot(
                from_imag, im_s[start : start + window], preferred_element_type=jnp.float32
            )
            real_part = acc[:tile]
            imag_part = acc[tile:]
            if step < steps - 1:
                re_t, im_t = turn_rows(
                    real_part.astype(jnp.bfloat16), imag_part.astype(jnp.bfloat16),
                    cos_all[step + 1], sin_all[step + 1],
                )
                re_s[start : start + tile] = re_t
                im_s[start : start + tile] = im_t
            else:
                o_ref[0, start : start + tile] = real_part
                o_ref[1, start : start + tile] = imag_part
                power = real_part * real_part + imag_part * imag_part
                folded = power[:, :lanes]
                for k in range(1, power.shape[1] // lanes):
                    folded = folded + power[:, k * lanes : (k + 1) * lanes]
                e_ref[start : start + tile] += folded
        rows_in -= tile


def compress_all(pieces, angles, weights):
    width = pieces[0].shape[2]
    rows = sum(piece.shape[1] for piece in pieces)
    blocks = weights.shape[0]
    bins = width // blocks
    steps = angles.shape[0]
    period = angles.shape[1]
    out_rows = rows - steps * weights.shape[-1]
    lanes = 128
    return pl.pallas_call(
        fused_kernel,
        grid=(blocks,),
        in_specs=[pl.BlockSpec((2, piece.shape[1], bins), lambda b: (0, 0, b)) for piece in pieces]
        + [
            pl.BlockSpec((steps, period, bins), lambda b: (0, 0, b)),
            pl.BlockSpec((1,) + weights.shape[1:], lambda b: (b, 0, 0, 0)),
        ],
        out_specs=[
            pl.BlockSpec((2, out_rows, bins), lambda b: (0, 0, b)),
            pl.BlockSpec((out_rows, lanes), lambda b: (0, 0)),
        ],
        out_shape=[
            jax.ShapeDtypeStruct((2, out_rows, width), jnp.float32),
            jax.ShapeDtypeStruct((out_rows, lanes), jnp.float32),
        ],
        scratch_shapes=[
            pltpu.VMEM((rows, bins), jnp.bfloat16),
            pltpu.VMEM((rows, bins), jnp.bfloat16),
        ],
        compiler_params=pltpu.CompilerParams(dimension_semantics=("arbitrary",)),
    )(*pieces, angles, weights)


def on_device(echo, nav_angles, owner, taps, band):
    filters = jnp.transpose(make_taps(taps, band).astype(jnp.float32), (1, 0, 2, 3))
    step_count = taps.shape[0]
    own = jnp.transpose(echo, (1, 0, 2))
    reach = step_count * (taps.shape[-1] // 2)
    assert reach == own.shape[1]
    mine, own_late, shapes = from_roots(
        nav_angles, "sector", [owner[step] for step in range(step_count)], own
    )
    left, right = exchange(own_late, own_late, "sector")
    all_angles = gather_roots(mine, "sector", shapes)
    result, partial = compress_all([left, own, right], all_angles, filters)
    energy = lax.psum(jnp.sum(partial, axis=1), "range")
    row_scale = lax.rsqrt(energy / (2.0 * RANGE) + 1e-05)
    scaled = (result * row_scale[None, :, None]).astype(jnp.bfloat16)
    return jnp.transpose(scaled, (1, 0, 2))


def solution(mesh):
    placed = (
        P("sector", None, "range"),
        P("sector", "range"),
        P(),
        P(None, "range", None, None),
        P("range"),
    )
    return jax.shard_map(
        on_device, mesh=mesh, in_specs=placed, out_specs=P("sector", None, "range"), check_vma=False
    )
```

```python
import functools

import jax
import jax.numpy as jnp
from jax import lax
from jax.experimental import pallas as pl
from jax.experimental.pallas import tpu as pltpu
from jax.sharding import PartitionSpec as P

RANGE = 8192


def from_roots(value, axis, sources, tied):
    count = lax.axis_size(axis)
    me = lax.axis_index(axis)
    kept = jnp.stack([jnp.where(me == source, value, 0) for source in sources]).astype(jnp.bfloat16)
    flat = kept.reshape(count, -1)
    part = lax.all_to_all(flat, axis, 0, 0, tiled=True)
    mine = jnp.sum(part, axis=0, keepdims=True)
    mine, tied = lax.optimization_barrier((mine, tied))
    return mine, tied, (flat.shape, kept.shape, value.dtype)


def gather_roots(mine, axis, shapes):
    flat_shape, kept_shape, dtype = shapes
    full = lax.all_to_all(jnp.broadcast_to(mine, flat_shape), axis, 0, 0, tiled=True)
    return full.reshape(kept_shape).astype(dtype)


def exchange(low_rows, high_rows, axis):
    count = lax.axis_size(axis)
    forward = [(i, (i + 1) % count) for i in range(count)]
    backward = [((i + 1) % count, i) for i in range(count)]
    low = lax.ppermute(high_rows, axis, forward)
    high = lax.ppermute(low_rows, axis, backward)
    return low, high


def make_taps(taps, band):
    taps_count = taps.shape[-1]
    half_taps = taps_count // 2
    offsets = jnp.arange(taps_count, dtype=jnp.int32) - half_taps
    band_col = band[:, None]
    inside = (offsets[None, :] >= -band_col) & (offsets[None, :] < band_col)
    band_gain = jnp.sqrt(half_taps / band.astype(jnp.float32))
    weighted = (
        taps.astype(jnp.float32)
        * inside[None, :, None, :].astype(jnp.float32)
        * band_gain[None, :, None, None]
    )
    return weighted.astype(jnp.bfloat16)


def turn_rows(re, im, cosine, sine):
    period = cosine.shape[0]
    rows, width = re.shape
    re = re.astype(jnp.float32).reshape(rows // period, period, width)
    im = im.astype(jnp.float32).reshape(rows // period, period, width)
    real_part = re * cosine[None] - im * sine[None]
    imag_part = re * sine[None] + im * cosine[None]
    return (
        real_part.reshape(rows, width).astype(jnp.bfloat16),
        imag_part.reshape(rows, width).astype(jnp.bfloat16),
    )


def toeplitz_rows(weights, window):
    taps = weights.shape[-1]
    base = jnp.concatenate(
        [jnp.broadcast_to(weights, (taps, taps)), jnp.zeros((taps, window - taps), weights.dtype)],
        axis=1,
    )
    return pltpu.roll(base, 0, 1, stride=1, stride_axis=0)


def fused_kernel(left_ref, own_ref, right_ref, a_ref, f_ref, o_ref, e_ref, re_s, im_s):
    angles = a_ref[...]
    cos_all = jnp.cos(angles)
    sin_all = jnp.sin(angles)
    steps = angles.shape[0]
    offset = 0
    for piece in (left_ref, own_ref, right_ref):
        rows = piece.shape[1]
        re_t, im_t = turn_rows(piece[0], piece[1], cos_all[0], sin_all[0])
        re_s[offset : offset + rows] = re_t
        im_s[offset : offset + rows] = im_t
        offset += rows

    @pl.when(pl.program_id(0) == 0)
    def _():
        e_ref[...] = jnp.zeros_like(e_ref)

    weights = f_ref[0]
    tile = weights.shape[-1]
    window = 2 * tile
    lanes = e_ref.shape[-1]
    rows_in = offset
    for step in range(steps):
        toep_real = toeplitz_rows(weights[step, 0:1], window)
        toep_imag = toeplitz_rows(weights[step, 1:2], window)
        from_real = jnp.concatenate([toep_real, toep_imag], axis=0).astype(jnp.bfloat16)
        from_imag = jnp.concatenate([-toep_imag, toep_real], axis=0).astype(jnp.bfloat16)
        for q in range(rows_in // tile - 1):
            start = q * tile
            acc = jnp.dot(
                from_real, re_s[start : start + window], preferred_element_type=jnp.float32
            )
            acc = acc + jnp.dot(
                from_imag, im_s[start : start + window], preferred_element_type=jnp.float32
            )
            real_part = acc[:tile]
            imag_part = acc[tile:]
            if step < steps - 1:
                re_t, im_t = turn_rows(
                    real_part.astype(jnp.bfloat16), imag_part.astype(jnp.bfloat16),
                    cos_all[step + 1], sin_all[step + 1],
                )
                re_s[start : start + tile] = re_t
                im_s[start : start + tile] = im_t
            else:
                o_ref[0, start : start + tile] = real_part
                o_ref[1, start : start + tile] = imag_part
                power = real_part * real_part + imag_part * imag_part
                folded = power[:, :lanes]
                for k in range(1, power.shape[1] // lanes):
                    folded = folded + power[:, k * lanes : (k + 1) * lanes]
                e_ref[start : start + tile] += folded
        rows_in -= tile


def compress_all(pieces, offsets, angles, angle_offset, weights, bins):
    blocks = weights.shape[0]
    width = blocks * bins
    rows = sum(piece.shape[1] for piece in pieces)
    steps = angles.shape[0]
    period = angles.shape[1]
    out_rows = rows - steps * weights.shape[-1]
    lanes = 128
    return pl.pallas_call(
        fused_kernel,
        grid=(blocks,),
        in_specs=[
            pl.BlockSpec((2, piece.shape[1], bins), lambda b, o=offset: (0, 0, b + o))
            for piece, offset in zip(pieces, offsets)
        ]
        + [
            pl.BlockSpec((steps, period, bins), lambda b: (0, 0, b + angle_offset)),
            pl.BlockSpec((1,) + weights.shape[1:], lambda b: (b, 0, 0, 0)),
        ],
        out_specs=[
            pl.BlockSpec((2, out_rows, bins), lambda b: (0, 0, b)),
            pl.BlockSpec((out_rows, lanes), lambda b: (0, 0)),
        ],
        out_shape=[
            jax.ShapeDtypeStruct((2, out_rows, width), jnp.float32),
            jax.ShapeDtypeStruct((out_rows, lanes), jnp.float32),
        ],
        scratch_shapes=[
            pltpu.VMEM((rows, bins), jnp.bfloat16),
            pltpu.VMEM((rows, bins), jnp.bfloat16),
        ],
        compiler_params=pltpu.CompilerParams(dimension_semantics=("arbitrary",)),
    )(*pieces, angles, weights)


def on_device(echo, nav_angles, owner, taps, band):
    filters = jnp.transpose(make_taps(taps, band).astype(jnp.float32), (1, 0, 2, 3))
    step_count = taps.shape[0]
    own = jnp.transpose(echo, (1, 0, 2))
    reach = step_count * (taps.shape[-1] // 2)
    assert reach == own.shape[1]
    blocks = filters.shape[0]
    half = blocks // 2
    bins = own.shape[2] // blocks
    cut = bins * half
    left_a, right_a = exchange(own[:, :, :cut], own[:, :, :cut], "sector")
    mine, _, shapes = from_roots(
        nav_angles, "sector", [owner[step] for step in range(step_count)], own
    )
    all_angles = gather_roots(mine, "sector", shapes)
    own_b, left_a, right_a, all_angles = lax.optimization_barrier(
        (own[:, :, cut:], left_a, right_a, all_angles)
    )
    left_b, right_b = exchange(own_b, own_b, "sector")
    result_a, partial_a = compress_all(
        [left_a, own, right_a], (0, 0, 0), all_angles, 0, filters[:half], bins
    )
    result_b, partial_b = compress_all(
        [left_b, own, right_b], (0, half, 0), all_angles, half, filters[half:], bins
    )
    result = jnp.concatenate([result_a, result_b], axis=2)
    partial = partial_a + partial_b
    energy = lax.psum(jnp.sum(partial, axis=1), "range")
    row_scale = lax.rsqrt(energy / (2.0 * RANGE) + 1e-05)
    scaled = (result * row_scale[None, :, None]).astype(jnp.bfloat16)
    return jnp.transpose(scaled, (1, 0, 2))


def solution(mesh):
    placed = (
        P("sector", None, "range"),
        P("sector", "range"),
        P(),
        P(None, "range", None, None),
        P("range"),
    )
    return jax.shard_map(
        on_device, mesh=mesh, in_specs=placed, out_specs=P("sector", None, "range"), check_vma=False
    )
```

```python
import functools

import jax
import jax.numpy as jnp
from jax import lax
from jax.experimental import pallas as pl
from jax.experimental.pallas import tpu as pltpu
from jax.sharding import PartitionSpec as P

RANGE = 8192


def from_roots(value, axis, sources, tied):
    count = lax.axis_size(axis)
    me = lax.axis_index(axis)
    kept = jnp.stack([jnp.where(me == source, value, 0) for source in sources]).astype(jnp.bfloat16)
    flat = kept.reshape(count, -1)
    part = lax.all_to_all(flat, axis, 0, 0, tiled=True)
    mine = jnp.sum(part, axis=0, keepdims=True)
    mine, tied = lax.optimization_barrier((mine, tied))
    return mine, tied, (flat.shape, kept.shape, value.dtype)


def gather_roots(mine, axis, shapes):
    flat_shape, kept_shape, dtype = shapes
    full = lax.all_to_all(jnp.broadcast_to(mine, flat_shape), axis, 0, 0, tiled=True)
    return full.reshape(kept_shape).astype(dtype)


def exchange(low_rows, high_rows, axis):
    count = lax.axis_size(axis)
    forward = [(i, (i + 1) % count) for i in range(count)]
    backward = [((i + 1) % count, i) for i in range(count)]
    low = lax.ppermute(high_rows, axis, forward)
    high = lax.ppermute(low_rows, axis, backward)
    return low, high


def make_taps(taps, band):
    taps_count = taps.shape[-1]
    half_taps = taps_count // 2
    offsets = jnp.arange(taps_count, dtype=jnp.int32) - half_taps
    band_col = band[:, None]
    inside = (offsets[None, :] >= -band_col) & (offsets[None, :] < band_col)
    band_gain = jnp.sqrt(half_taps / band.astype(jnp.float32))
    weighted = (
        taps.astype(jnp.float32)
        * inside[None, :, None, :].astype(jnp.float32)
        * band_gain[None, :, None, None]
    )
    return weighted.astype(jnp.bfloat16)


def turn_rows(re, im, cosine, sine):
    period = cosine.shape[0]
    rows, width = re.shape
    re = re.astype(jnp.float32).reshape(rows // period, period, width)
    im = im.astype(jnp.float32).reshape(rows // period, period, width)
    real_part = re * cosine[None] - im * sine[None]
    imag_part = re * sine[None] + im * cosine[None]
    return (
        real_part.reshape(rows, width).astype(jnp.bfloat16),
        imag_part.reshape(rows, width).astype(jnp.bfloat16),
    )


def toeplitz_rows(weights, window):
    taps = weights.shape[-1]
    base = jnp.concatenate(
        [jnp.broadcast_to(weights, (taps, taps)), jnp.zeros((taps, window - taps), weights.dtype)],
        axis=1,
    )
    return pltpu.roll(base, 0, 1, stride=1, stride_axis=0)


def fused_kernel(left_ref, own_ref, right_ref, a_ref, f_ref, o_ref, e_ref, re_s, im_s):
    angles = a_ref[...]
    cos_all = jnp.cos(angles)
    sin_all = jnp.sin(angles)
    steps = angles.shape[0]
    offset = 0
    for piece in (left_ref, own_ref, right_ref):
        rows = piece.shape[1]
        re_t, im_t = turn_rows(piece[0], piece[1], cos_all[0], sin_all[0])
        re_s[offset : offset + rows] = re_t
        im_s[offset : offset + rows] = im_t
        offset += rows

    @pl.when(pl.program_id(0) == 0)
    def _():
        e_ref[...] = jnp.zeros_like(e_ref)

    weights = f_ref[0]
    tile = weights.shape[-1]
    window = 2 * tile
    lanes = e_ref.shape[-1]
    rows_in = offset
    for step in range(steps):
        toep_real = toeplitz_rows(weights[step, 0:1], window)
        toep_imag = toeplitz_rows(weights[step, 1:2], window)
        from_real = jnp.concatenate([toep_real, toep_imag], axis=0).astype(jnp.bfloat16)
        from_imag = jnp.concatenate([-toep_imag, toep_real], axis=0).astype(jnp.bfloat16)
        for q in range(rows_in // tile - 1):
            start = q * tile
            acc = jnp.dot(
                from_real, re_s[start : start + window], preferred_element_type=jnp.float32
            )
            acc = acc + jnp.dot(
                from_imag, im_s[start : start + window], preferred_element_type=jnp.float32
            )
            real_part = acc[:tile]
            imag_part = acc[tile:]
            if step < steps - 1:
                re_t, im_t = turn_rows(
                    real_part.astype(jnp.bfloat16), imag_part.astype(jnp.bfloat16),
                    cos_all[step + 1], sin_all[step + 1],
                )
                re_s[start : start + tile] = re_t
                im_s[start : start + tile] = im_t
            else:
                o_ref[0, start : start + tile] = real_part
                o_ref[1, start : start + tile] = imag_part
                power = real_part * real_part + imag_part * imag_part
                folded = power[:, :lanes]
                for k in range(1, power.shape[1] // lanes):
                    folded = folded + power[:, k * lanes : (k + 1) * lanes]
                e_ref[start : start + tile] += folded
        rows_in -= tile


def compress_all(pieces, offsets, angles, angle_offset, weights, bins):
    blocks = weights.shape[0]
    width = blocks * bins
    rows = sum(piece.shape[1] for piece in pieces)
    steps = angles.shape[0]
    period = angles.shape[1]
    out_rows = rows - steps * weights.shape[-1]
    lanes = 128
    return pl.pallas_call(
        fused_kernel,
        grid=(blocks,),
        in_specs=[
            pl.BlockSpec((2, piece.shape[1], bins), lambda b, o=offset: (0, 0, b + o))
            for piece, offset in zip(pieces, offsets)
        ]
        + [
            pl.BlockSpec((steps, period, bins), lambda b: (0, 0, b + angle_offset)),
            pl.BlockSpec((1,) + weights.shape[1:], lambda b: (b, 0, 0, 0)),
        ],
        out_specs=[
            pl.BlockSpec((2, out_rows, bins), lambda b: (0, 0, b)),
            pl.BlockSpec((out_rows, lanes), lambda b: (0, 0)),
        ],
        out_shape=[
            jax.ShapeDtypeStruct((2, out_rows, width), jnp.float32),
            jax.ShapeDtypeStruct((out_rows, lanes), jnp.float32),
        ],
        scratch_shapes=[
            pltpu.VMEM((rows, bins), jnp.bfloat16),
            pltpu.VMEM((rows, bins), jnp.bfloat16),
        ],
        compiler_params=pltpu.CompilerParams(dimension_semantics=("arbitrary",)),
    )(*pieces, angles, weights)


def on_device(echo, nav_angles, owner, taps, band):
    filters = jnp.transpose(make_taps(taps, band).astype(jnp.float32), (1, 0, 2, 3))
    step_count = taps.shape[0]
    own = jnp.transpose(echo, (1, 0, 2))
    reach = step_count * (taps.shape[-1] // 2)
    assert reach == own.shape[1]
    blocks = filters.shape[0]
    half = blocks * 3 // 4
    bins = own.shape[2] // blocks
    cut = bins * half
    left_a, right_a = exchange(own[:, :, :cut], own[:, :, :cut], "sector")
    mine, _, shapes = from_roots(
        nav_angles, "sector", [owner[step] for step in range(step_count)], own
    )
    all_angles = gather_roots(mine, "sector", shapes)
    own_b, left_a, right_a, all_angles = lax.optimization_barrier(
        (own[:, :, cut:], left_a, right_a, all_angles)
    )
    left_b, right_b = exchange(own_b, own_b, "sector")
    result_a, partial_a = compress_all(
        [left_a, own, right_a], (0, 0, 0), all_angles, 0, filters[:half], bins
    )
    result_b, partial_b = compress_all(
        [left_b, own, right_b], (0, half, 0), all_angles, half, filters[half:], bins
    )
    result = jnp.concatenate([result_a, result_b], axis=2)
    partial = partial_a + partial_b
    energy = lax.psum(jnp.sum(partial, axis=1), "range")
    row_scale = lax.rsqrt(energy / (2.0 * RANGE) + 1e-05)
    scaled = (result * row_scale[None, :, None]).astype(jnp.bfloat16)
    return jnp.transpose(scaled, (1, 0, 2))


def solution(mesh):
    placed = (
        P("sector", None, "range"),
        P("sector", "range"),
        P(),
        P(None, "range", None, None),
        P("range"),
    )
    return jax.shard_map(
        on_device, mesh=mesh, in_specs=placed, out_specs=P("sector", None, "range"), check_vma=False
    )
```

```python
import functools

import jax
import jax.numpy as jnp
from jax import lax
from jax.experimental import pallas as pl
from jax.experimental.pallas import tpu as pltpu
from jax.sharding import PartitionSpec as P

RANGE = 8192


def from_roots(value, axis, sources, tied):
    count = lax.axis_size(axis)
    me = lax.axis_index(axis)
    kept = jnp.stack([jnp.where(me == source, value, 0) for source in sources]).astype(jnp.bfloat16)
    flat = kept.reshape(count, -1)
    part = lax.all_to_all(flat, axis, 0, 0, tiled=True)
    mine = jnp.sum(part, axis=0, keepdims=True)
    mine, tied = lax.optimization_barrier((mine, tied))
    return mine, tied, (flat.shape, kept.shape, value.dtype)


def gather_roots(mine, axis, shapes):
    flat_shape, kept_shape, dtype = shapes
    full = lax.all_to_all(jnp.broadcast_to(mine, flat_shape), axis, 0, 0, tiled=True)
    return full.reshape(kept_shape).astype(dtype)


def exchange(low_rows, high_rows, axis):
    count = lax.axis_size(axis)
    forward = [(i, (i + 1) % count) for i in range(count)]
    backward = [((i + 1) % count, i) for i in range(count)]
    low = lax.ppermute(high_rows, axis, forward)
    high = lax.ppermute(low_rows, axis, backward)
    return low, high


def make_taps(taps, band):
    taps_count = taps.shape[-1]
    half_taps = taps_count // 2
    offsets = jnp.arange(taps_count, dtype=jnp.int32) - half_taps
    band_col = band[:, None]
    inside = (offsets[None, :] >= -band_col) & (offsets[None, :] < band_col)
    band_gain = jnp.sqrt(half_taps / band.astype(jnp.float32))
    weighted = (
        taps.astype(jnp.float32)
        * inside[None, :, None, :].astype(jnp.float32)
        * band_gain[None, :, None, None]
    )
    return weighted.astype(jnp.bfloat16)


def turn_rows(re, im, cosine, sine):
    period = cosine.shape[0]
    rows, width = re.shape
    re = re.astype(jnp.float32).reshape(rows // period, period, width)
    im = im.astype(jnp.float32).reshape(rows // period, period, width)
    real_part = re * cosine[None] - im * sine[None]
    imag_part = re * sine[None] + im * cosine[None]
    return (
        real_part.reshape(rows, width).astype(jnp.bfloat16),
        imag_part.reshape(rows, width).astype(jnp.bfloat16),
    )


def toeplitz_rows(weights, window):
    taps = weights.shape[-1]
    base = jnp.concatenate(
        [jnp.broadcast_to(weights, (taps, taps)), jnp.zeros((taps, window - taps), weights.dtype)],
        axis=1,
    )
    return pltpu.roll(base, 0, 1, stride=1, stride_axis=0)


def fused_kernel(left_ref, own_ref, right_ref, a_ref, f_ref, o_ref, e_ref, re_s, im_s):
    angles = a_ref[...]
    cos_all = jnp.cos(angles)
    sin_all = jnp.sin(angles)
    steps = angles.shape[0]
    offset = 0
    for piece in (left_ref, own_ref, right_ref):
        rows = piece.shape[1]
        re_t, im_t = turn_rows(piece[0], piece[1], cos_all[0], sin_all[0])
        re_s[offset : offset + rows] = re_t
        im_s[offset : offset + rows] = im_t
        offset += rows

    @pl.when(pl.program_id(0) == 0)
    def _():
        e_ref[...] = jnp.zeros_like(e_ref)

    weights = f_ref[0]
    tile = weights.shape[-1]
    window = 2 * tile
    lanes = e_ref.shape[-1]
    rows_in = offset
    for step in range(steps):
        toep_real = toeplitz_rows(weights[step, 0:1], window)
        toep_imag = toeplitz_rows(weights[step, 1:2], window)
        from_real = jnp.concatenate([toep_real, toep_imag], axis=0).astype(jnp.bfloat16)
        from_imag = jnp.concatenate([-toep_imag, toep_real], axis=0).astype(jnp.bfloat16)
        for q in range(rows_in // tile - 1):
            start = q * tile
            acc = jnp.dot(
                from_real, re_s[start : start + window], preferred_element_type=jnp.float32
            )
            acc = acc + jnp.dot(
                from_imag, im_s[start : start + window], preferred_element_type=jnp.float32
            )
            real_part = acc[:tile]
            imag_part = acc[tile:]
            if step < steps - 1:
                re_t, im_t = turn_rows(
                    real_part.astype(jnp.bfloat16), imag_part.astype(jnp.bfloat16),
                    cos_all[step + 1], sin_all[step + 1],
                )
                re_s[start : start + tile] = re_t
                im_s[start : start + tile] = im_t
            else:
                o_ref[0, start : start + tile] = real_part
                o_ref[1, start : start + tile] = imag_part
                power = real_part * real_part + imag_part * imag_part
                folded = power[:, :lanes]
                for k in range(1, power.shape[1] // lanes):
                    folded = folded + power[:, k * lanes : (k + 1) * lanes]
                e_ref[start : start + tile] += folded
        rows_in -= tile


def compress_all(pieces, offsets, angles, angle_offset, weights, bins):
    blocks = weights.shape[0]
    width = blocks * bins
    rows = sum(piece.shape[1] for piece in pieces)
    steps = angles.shape[0]
    period = angles.shape[1]
    out_rows = rows - steps * weights.shape[-1]
    lanes = 128
    return pl.pallas_call(
        fused_kernel,
        grid=(blocks,),
        in_specs=[
            pl.BlockSpec((2, piece.shape[1], bins), lambda b, o=offset: (0, 0, b + o))
            for piece, offset in zip(pieces, offsets)
        ]
        + [
            pl.BlockSpec((steps, period, bins), lambda b: (0, 0, b + angle_offset)),
            pl.BlockSpec((1,) + weights.shape[1:], lambda b: (b, 0, 0, 0)),
        ],
        out_specs=[
            pl.BlockSpec((2, out_rows, bins), lambda b: (0, 0, b)),
            pl.BlockSpec((out_rows, lanes), lambda b: (0, 0)),
        ],
        out_shape=[
            jax.ShapeDtypeStruct((2, out_rows, width), jnp.float32),
            jax.ShapeDtypeStruct((out_rows, lanes), jnp.float32),
        ],
        scratch_shapes=[
            pltpu.VMEM((rows, bins), jnp.bfloat16),
            pltpu.VMEM((rows, bins), jnp.bfloat16),
        ],
        compiler_params=pltpu.CompilerParams(dimension_semantics=("arbitrary",)),
    )(*pieces, angles, weights)


def on_device(echo, nav_angles, owner, taps, band):
    filters = jnp.transpose(make_taps(taps, band).astype(jnp.float32), (1, 0, 2, 3))
    step_count = taps.shape[0]
    own = jnp.transpose(echo, (1, 0, 2))
    reach = step_count * (taps.shape[-1] // 2)
    assert reach == own.shape[1]
    blocks = filters.shape[0]
    half = blocks * 3 // 4
    bins = own.shape[2] // blocks
    cut = bins * half
    left_a, right_a = exchange(own[:, :, :cut], own[:, :, :cut], "sector")
    mine, _, shapes = from_roots(
        nav_angles, "sector", [owner[step] for step in range(step_count)], own
    )
    all_angles = gather_roots(mine, "sector", shapes)
    own_b, left_a, right_a, all_angles = lax.optimization_barrier(
        (own[:, :, cut:], left_a, right_a, all_angles)
    )
    left_b, right_b = exchange(own_b, own_b, "sector")
    result_a, partial_a = compress_all(
        [left_a, own, right_a], (0, 0, 0), all_angles, 0, filters[:half], bins
    )
    result_b, partial_b = compress_all(
        [left_b, own, right_b], (0, half, 0), all_angles, half, filters[half:], bins
    )
    result = jnp.concatenate([result_a, result_b], axis=2)
    partial = partial_a + partial_b
    partial = jnp.sum(partial, axis=1)
    count = lax.axis_size("range")
    shared = jnp.broadcast_to(partial[None], (count,) + partial.shape)
    energy = jnp.sum(lax.all_to_all(shared, "range", 0, 0, tiled=True), axis=0)
    row_scale = lax.rsqrt(energy / (2.0 * RANGE) + 1e-05)
    scaled = (result * row_scale[None, :, None]).astype(jnp.bfloat16)
    return jnp.transpose(scaled, (1, 0, 2))


def solution(mesh):
    placed = (
        P("sector", None, "range"),
        P("sector", "range"),
        P(),
        P(None, "range", None, None),
        P("range"),
    )
    return jax.shard_map(
        on_device, mesh=mesh, in_specs=placed, out_specs=P("sector", None, "range"), check_vma=False
    )
```

```python
import functools

import jax
import jax.numpy as jnp
from jax import lax
from jax.experimental import pallas as pl
from jax.experimental.pallas import tpu as pltpu
from jax.sharding import PartitionSpec as P

RANGE = 8192


def from_roots(value, axis, sources, tied):
    count = lax.axis_size(axis)
    me = lax.axis_index(axis)
    kept = jnp.stack([jnp.where(me == source, value, 0) for source in sources]).astype(jnp.bfloat16)
    flat = kept.reshape(count, -1)
    part = lax.all_to_all(flat, axis, 0, 0, tiled=True)
    mine = jnp.sum(part, axis=0, keepdims=True)
    mine, tied = lax.optimization_barrier((mine, tied))
    return mine, tied, (flat.shape, kept.shape, value.dtype)


def gather_roots(mine, axis, shapes):
    flat_shape, kept_shape, dtype = shapes
    full = lax.all_to_all(jnp.broadcast_to(mine, flat_shape), axis, 0, 0, tiled=True)
    return full.reshape(kept_shape).astype(dtype)


def exchange(low_rows, high_rows, axis):
    count = lax.axis_size(axis)
    forward = [(i, (i + 1) % count) for i in range(count)]
    backward = [((i + 1) % count, i) for i in range(count)]
    low = lax.ppermute(high_rows, axis, forward)
    high = lax.ppermute(low_rows, axis, backward)
    return low, high


def make_taps(taps, band):
    taps_count = taps.shape[-1]
    half_taps = taps_count // 2
    offsets = jnp.arange(taps_count, dtype=jnp.int32) - half_taps
    band_col = band[:, None]
    inside = (offsets[None, :] >= -band_col) & (offsets[None, :] < band_col)
    band_gain = jnp.sqrt(half_taps / band.astype(jnp.float32))
    weighted = (
        taps.astype(jnp.float32)
        * inside[None, :, None, :].astype(jnp.float32)
        * band_gain[None, :, None, None]
    )
    return weighted.astype(jnp.bfloat16)


def turn_rows(re, im, cosine, sine):
    period = cosine.shape[0]
    rows, width = re.shape
    re = re.astype(jnp.float32).reshape(rows // period, period, width)
    im = im.astype(jnp.float32).reshape(rows // period, period, width)
    real_part = re * cosine[None] - im * sine[None]
    imag_part = re * sine[None] + im * cosine[None]
    return (
        real_part.reshape(rows, width).astype(jnp.bfloat16),
        imag_part.reshape(rows, width).astype(jnp.bfloat16),
    )


def toeplitz_rows(weights, window):
    taps = weights.shape[-1]
    base = jnp.concatenate(
        [jnp.broadcast_to(weights, (taps, taps)), jnp.zeros((taps, window - taps), weights.dtype)],
        axis=1,
    )
    return pltpu.roll(base, 0, 1, stride=1, stride_axis=0)


def fused_kernel(left_ref, own_ref, right_ref, a_ref, f_ref, o_ref, e_ref, re_s, im_s):
    angles = a_ref[...]
    cos_all = jnp.cos(angles)
    sin_all = jnp.sin(angles)
    steps = angles.shape[0]
    offset = 0
    for piece in (left_ref, own_ref, right_ref):
        rows = piece.shape[1]
        re_t, im_t = turn_rows(piece[0], piece[1], cos_all[0], sin_all[0])
        re_s[offset : offset + rows] = re_t
        im_s[offset : offset + rows] = im_t
        offset += rows

    @pl.when(pl.program_id(0) == 0)
    def _():
        e_ref[...] = jnp.zeros_like(e_ref)

    weights = f_ref[0]
    tile = weights.shape[-1]
    window = 2 * tile
    lanes = e_ref.shape[-1]
    rows_in = offset
    for step in range(steps):
        toep_real = toeplitz_rows(weights[step, 0:1], window)
        toep_imag = toeplitz_rows(weights[step, 1:2], window)
        from_real = jnp.concatenate([toep_real, toep_imag], axis=0).astype(jnp.bfloat16)
        from_imag = jnp.concatenate([-toep_imag, toep_real], axis=0).astype(jnp.bfloat16)
        for q in range(rows_in // tile - 1):
            start = q * tile
            acc = jnp.dot(
                from_real, re_s[start : start + window], preferred_element_type=jnp.float32
            )
            acc = acc + jnp.dot(
                from_imag, im_s[start : start + window], preferred_element_type=jnp.float32
            )
            real_part = acc[:tile]
            imag_part = acc[tile:]
            if step < steps - 1:
                re_t, im_t = turn_rows(
                    real_part.astype(jnp.bfloat16), imag_part.astype(jnp.bfloat16),
                    cos_all[step + 1], sin_all[step + 1],
                )
                re_s[start : start + tile] = re_t
                im_s[start : start + tile] = im_t
            else:
                o_ref[0, start : start + tile] = real_part
                o_ref[1, start : start + tile] = imag_part
                power = real_part * real_part + imag_part * imag_part
                folded = power[:, :lanes]
                for k in range(1, power.shape[1] // lanes):
                    folded = folded + power[:, k * lanes : (k + 1) * lanes]
                e_ref[start : start + tile] += folded
        rows_in -= tile


def compress_all(pieces, offsets, angles, angle_offset, weights, bins):
    blocks = weights.shape[0]
    width = blocks * bins
    rows = sum(piece.shape[1] for piece in pieces)
    steps = angles.shape[0]
    period = angles.shape[1]
    out_rows = rows - steps * weights.shape[-1]
    lanes = 128
    return pl.pallas_call(
        fused_kernel,
        grid=(blocks,),
        in_specs=[
            pl.BlockSpec((2, piece.shape[1], bins), lambda b, o=offset: (0, 0, b + o))
            for piece, offset in zip(pieces, offsets)
        ]
        + [
            pl.BlockSpec((steps, period, bins), lambda b: (0, 0, b + angle_offset)),
            pl.BlockSpec((1,) + weights.shape[1:], lambda b: (b, 0, 0, 0)),
        ],
        out_specs=[
            pl.BlockSpec((2, out_rows, bins), lambda b: (0, 0, b)),
            pl.BlockSpec((out_rows, lanes), lambda b: (0, 0)),
        ],
        out_shape=[
            jax.ShapeDtypeStruct((2, out_rows, width), jnp.float32),
            jax.ShapeDtypeStruct((out_rows, lanes), jnp.float32),
        ],
        scratch_shapes=[
            pltpu.VMEM((rows, bins), jnp.bfloat16),
            pltpu.VMEM((rows, bins), jnp.bfloat16),
        ],
        compiler_params=pltpu.CompilerParams(dimension_semantics=("arbitrary",)),
    )(*pieces, angles, weights)


def on_device(echo, nav_angles, owner, taps, band):
    filters = jnp.transpose(make_taps(taps, band).astype(jnp.float32), (1, 0, 2, 3))
    step_count = taps.shape[0]
    blocks = filters.shape[0]
    half = blocks * 3 // 4
    bins = echo.shape[2] // blocks
    cut = bins * half
    own_a = jnp.transpose(echo[:, :, :cut], (1, 0, 2))
    own_b = jnp.transpose(echo[:, :, cut:], (1, 0, 2))
    reach = step_count * (taps.shape[-1] // 2)
    assert reach == own_a.shape[1]
    left_a, right_a = exchange(own_a, own_a, "sector")
    mine, _, shapes = from_roots(
        nav_angles, "sector", [owner[step] for step in range(step_count)], own_a
    )
    all_angles = gather_roots(mine, "sector", shapes)
    own_b, left_a, right_a, all_angles = lax.optimization_barrier(
        (own_b, left_a, right_a, all_angles)
    )
    left_b, right_b = exchange(own_b, own_b, "sector")
    result_a, partial_a = compress_all(
        [left_a, own_a, right_a], (0, 0, 0), all_angles, 0, filters[:half], bins
    )
    result_b, partial_b = compress_all(
        [left_b, own_b, right_b], (0, 0, 0), all_angles, half, filters[half:], bins
    )
    result = jnp.concatenate([result_a, result_b], axis=2)
    partial = partial_a + partial_b
    energy = lax.psum(jnp.sum(partial, axis=1), "range")
    row_scale = lax.rsqrt(energy / (2.0 * RANGE) + 1e-05)
    scaled = (result * row_scale[None, :, None]).astype(jnp.bfloat16)
    return jnp.transpose(scaled, (1, 0, 2))


def solution(mesh):
    placed = (
        P("sector", None, "range"),
        P("sector", "range"),
        P(),
        P(None, "range", None, None),
        P("range"),
    )
    return jax.shard_map(
        on_device, mesh=mesh, in_specs=placed, out_specs=P("sector", None, "range"), check_vma=False
    )
```

```python
import functools

import jax
import jax.numpy as jnp
from jax import lax
from jax.experimental import pallas as pl
from jax.experimental.pallas import tpu as pltpu
from jax.sharding import PartitionSpec as P

RANGE = 8192


def from_roots(value, axis, sources, tied):
    count = lax.axis_size(axis)
    me = lax.axis_index(axis)
    kept = jnp.stack([jnp.where(me == source, value, 0) for source in sources]).astype(jnp.bfloat16)
    flat = kept.reshape(count, -1)
    part = lax.all_to_all(flat, axis, 0, 0, tiled=True)
    mine = jnp.sum(part, axis=0, keepdims=True)
    mine, tied = lax.optimization_barrier((mine, tied))
    return mine, tied, (flat.shape, kept.shape, value.dtype)


def gather_roots(mine, axis, shapes):
    flat_shape, kept_shape, dtype = shapes
    full = lax.all_to_all(jnp.broadcast_to(mine, flat_shape), axis, 0, 0, tiled=True)
    return full.reshape(kept_shape).astype(dtype)


def exchange(low_rows, high_rows, axis):
    count = lax.axis_size(axis)
    forward = [(i, (i + 1) % count) for i in range(count)]
    backward = [((i + 1) % count, i) for i in range(count)]
    low = lax.ppermute(high_rows, axis, forward)
    high = lax.ppermute(low_rows, axis, backward)
    return low, high


def make_taps(taps, band):
    taps_count = taps.shape[-1]
    half_taps = taps_count // 2
    offsets = jnp.arange(taps_count, dtype=jnp.int32) - half_taps
    band_col = band[:, None]
    inside = (offsets[None, :] >= -band_col) & (offsets[None, :] < band_col)
    band_gain = jnp.sqrt(half_taps / band.astype(jnp.float32))
    weighted = (
        taps.astype(jnp.float32)
        * inside[None, :, None, :].astype(jnp.float32)
        * band_gain[None, :, None, None]
    )
    return weighted.astype(jnp.bfloat16)


def turn_rows(re, im, cosine, sine):
    period = cosine.shape[0]
    rows, width = re.shape
    re = re.astype(jnp.float32).reshape(rows // period, period, width)
    im = im.astype(jnp.float32).reshape(rows // period, period, width)
    real_part = re * cosine[None] - im * sine[None]
    imag_part = re * sine[None] + im * cosine[None]
    return (
        real_part.reshape(rows, width).astype(jnp.bfloat16),
        imag_part.reshape(rows, width).astype(jnp.bfloat16),
    )


def toeplitz_rows(weights, window):
    taps = weights.shape[-1]
    base = jnp.concatenate(
        [jnp.broadcast_to(weights, (taps, taps)), jnp.zeros((taps, window - taps), weights.dtype)],
        axis=1,
    )
    return pltpu.roll(base, 0, 1, stride=1, stride_axis=0)


def fused_kernel(left_ref, own_ref, right_ref, a_ref, f_ref, o_ref, e_ref, re_s, im_s):
    angles = a_ref[...]
    cos_all = jnp.cos(angles)
    sin_all = jnp.sin(angles)
    steps = angles.shape[0]
    offset = 0
    for piece in (left_ref, own_ref, right_ref):
        rows = piece.shape[1]
        re_t, im_t = turn_rows(piece[0], piece[1], cos_all[0], sin_all[0])
        re_s[offset : offset + rows] = re_t
        im_s[offset : offset + rows] = im_t
        offset += rows

    @pl.when(pl.program_id(0) == 0)
    def _():
        e_ref[...] = jnp.zeros_like(e_ref)

    weights = f_ref[0]
    tile = weights.shape[-1]
    window = 2 * tile
    lanes = e_ref.shape[-1]
    rows_in = offset
    for step in range(steps):
        toep_real = toeplitz_rows(weights[step, 0:1], window)
        toep_imag = toeplitz_rows(weights[step, 1:2], window)
        from_real = jnp.concatenate([toep_real, toep_imag], axis=0).astype(jnp.bfloat16)
        from_imag = jnp.concatenate([-toep_imag, toep_real], axis=0).astype(jnp.bfloat16)
        for q in range(rows_in // tile - 1):
            start = q * tile
            acc = jnp.dot(
                from_real, re_s[start : start + window], preferred_element_type=jnp.float32
            )
            acc = acc + jnp.dot(
                from_imag, im_s[start : start + window], preferred_element_type=jnp.float32
            )
            real_part = acc[:tile]
            imag_part = acc[tile:]
            if step < steps - 1:
                re_t, im_t = turn_rows(
                    real_part.astype(jnp.bfloat16), imag_part.astype(jnp.bfloat16),
                    cos_all[step + 1], sin_all[step + 1],
                )
                re_s[start : start + tile] = re_t
                im_s[start : start + tile] = im_t
            else:
                o_ref[0, start : start + tile] = real_part
                o_ref[1, start : start + tile] = imag_part
                power = real_part * real_part + imag_part * imag_part
                folded = power[:, :lanes]
                for k in range(1, power.shape[1] // lanes):
                    folded = folded + power[:, k * lanes : (k + 1) * lanes]
                e_ref[start : start + tile] += folded
        rows_in -= tile


def compress_all(pieces, offsets, angles, angle_offset, weights, bins):
    blocks = weights.shape[0]
    width = blocks * bins
    rows = sum(piece.shape[1] for piece in pieces)
    steps = angles.shape[0]
    period = angles.shape[1]
    out_rows = rows - steps * weights.shape[-1]
    lanes = 128
    return pl.pallas_call(
        fused_kernel,
        grid=(blocks,),
        in_specs=[
            pl.BlockSpec((2, piece.shape[1], bins), lambda b, o=offset: (0, 0, b + o))
            for piece, offset in zip(pieces, offsets)
        ]
        + [
            pl.BlockSpec((steps, period, bins), lambda b: (0, 0, b + angle_offset)),
            pl.BlockSpec((1,) + weights.shape[1:], lambda b: (b, 0, 0, 0)),
        ],
        out_specs=[
            pl.BlockSpec((2, out_rows, bins), lambda b: (0, 0, b)),
            pl.BlockSpec((out_rows, lanes), lambda b: (0, 0)),
        ],
        out_shape=[
            jax.ShapeDtypeStruct((2, out_rows, width), jnp.float32),
            jax.ShapeDtypeStruct((out_rows, lanes), jnp.float32),
        ],
        scratch_shapes=[
            pltpu.VMEM((rows, bins), jnp.bfloat16),
            pltpu.VMEM((rows, bins), jnp.bfloat16),
        ],
        compiler_params=pltpu.CompilerParams(dimension_semantics=("arbitrary",)),
    )(*pieces, angles, weights)


def on_device(echo, nav_angles, owner, taps, band):
    filters = jnp.transpose(make_taps(taps, band).astype(jnp.float32), (1, 0, 2, 3))
    step_count = taps.shape[0]
    own = jnp.transpose(echo, (1, 0, 2))
    reach = step_count * (taps.shape[-1] // 2)
    assert reach == own.shape[1]
    blocks = filters.shape[0]
    bins = own.shape[2] // blocks
    sizes = [blocks * 5 // 8, blocks * 2 // 8]
    sizes.append(blocks - sum(sizes))
    starts = [sum(sizes[:k]) for k in range(len(sizes))]
    first = own[:, :, : sizes[0] * bins]
    halos = [exchange(first, first, "sector")]
    mine, _, shapes = from_roots(
        nav_angles, "sector", [owner[step] for step in range(step_count)], own
    )
    all_angles = gather_roots(mine, "sector", shapes)
    results = []
    partial = None
    for k in range(len(sizes)):
        if k + 1 < len(sizes):
            chunk = own[:, :, starts[k + 1] * bins : (starts[k + 1] + sizes[k + 1]) * bins]
            tie = (all_angles,) if k == 0 else (results[-1],)
            chunk, previous, tie = lax.optimization_barrier((chunk, halos[-1], tie))
            halos[-1] = previous
            if k == 0:
                (all_angles,) = tie
            else:
                results[-1] = tie[0]
            halos.append(exchange(chunk, chunk, "sector"))
        left, right = halos[k]
        result_k, partial_k = compress_all(
            [left, own, right], (0, starts[k], 0), all_angles, starts[k],
            filters[starts[k] : starts[k] + sizes[k]], bins,
        )
        results.append(result_k)
        partial = partial_k if partial is None else partial + partial_k
    result = jnp.concatenate(results, axis=2)
    energy = lax.psum(jnp.sum(partial, axis=1), "range")
    row_scale = lax.rsqrt(energy / (2.0 * RANGE) + 1e-05)
    scaled = (result * row_scale[None, :, None]).astype(jnp.bfloat16)
    return jnp.transpose(scaled, (1, 0, 2))


def solution(mesh):
    placed = (
        P("sector", None, "range"),
        P("sector", "range"),
        P(),
        P(None, "range", None, None),
        P("range"),
    )
    return jax.shard_map(
        on_device, mesh=mesh, in_specs=placed, out_specs=P("sector", None, "range"), check_vma=False
    )
```

```python
import functools

import jax
import jax.numpy as jnp
from jax import lax
from jax.experimental import pallas as pl
from jax.experimental.pallas import tpu as pltpu
from jax.sharding import PartitionSpec as P

RANGE = 8192


def from_roots(value, axis, sources, tied):
    count = lax.axis_size(axis)
    me = lax.axis_index(axis)
    kept = jnp.stack([jnp.where(me == source, value, 0) for source in sources]).astype(jnp.bfloat16)
    flat = kept.reshape(count, -1)
    part = lax.all_to_all(flat, axis, 0, 0, tiled=True)
    mine = jnp.sum(part, axis=0, keepdims=True)
    mine, tied = lax.optimization_barrier((mine, tied))
    return mine, tied, (flat.shape, kept.shape, value.dtype)


def gather_roots(mine, axis, shapes):
    flat_shape, kept_shape, dtype = shapes
    full = lax.all_to_all(jnp.broadcast_to(mine, flat_shape), axis, 0, 0, tiled=True)
    return full.reshape(kept_shape).astype(dtype)


def exchange(low_rows, high_rows, axis):
    count = lax.axis_size(axis)
    forward = [(i, (i + 1) % count) for i in range(count)]
    backward = [((i + 1) % count, i) for i in range(count)]
    low = lax.ppermute(high_rows, axis, forward)
    high = lax.ppermute(low_rows, axis, backward)
    return low, high


def make_taps(taps, band):
    taps_count = taps.shape[-1]
    half_taps = taps_count // 2
    offsets = jnp.arange(taps_count, dtype=jnp.int32) - half_taps
    band_col = band[:, None]
    inside = (offsets[None, :] >= -band_col) & (offsets[None, :] < band_col)
    band_gain = jnp.sqrt(half_taps / band.astype(jnp.float32))
    weighted = (
        taps.astype(jnp.float32)
        * inside[None, :, None, :].astype(jnp.float32)
        * band_gain[None, :, None, None]
    )
    return weighted.astype(jnp.bfloat16)


def turn_rows(re, im, cosine, sine):
    period = cosine.shape[0]
    rows, width = re.shape
    re = re.astype(jnp.float32).reshape(rows // period, period, width)
    im = im.astype(jnp.float32).reshape(rows // period, period, width)
    real_part = re * cosine[None] - im * sine[None]
    imag_part = re * sine[None] + im * cosine[None]
    return (
        real_part.reshape(rows, width).astype(jnp.bfloat16),
        imag_part.reshape(rows, width).astype(jnp.bfloat16),
    )


def toeplitz_rows(weights, window):
    taps = weights.shape[-1]
    base = jnp.concatenate(
        [jnp.broadcast_to(weights, (taps, taps)), jnp.zeros((taps, window - taps), weights.dtype)],
        axis=1,
    )
    return pltpu.roll(base, 0, 1, stride=1, stride_axis=0)


def fused_kernel(left_ref, own_ref, right_ref, a_ref, f_ref, o_ref, e_ref, re_s, im_s):
    angles = a_ref[...]
    cos_all = jnp.cos(angles)
    sin_all = jnp.sin(angles)
    steps = angles.shape[0]
    offset = 0
    for piece in (left_ref, own_ref, right_ref):
        rows = piece.shape[1]
        re_t, im_t = turn_rows(piece[0], piece[1], cos_all[0], sin_all[0])
        re_s[offset : offset + rows] = re_t
        im_s[offset : offset + rows] = im_t
        offset += rows

    @pl.when(pl.program_id(0) == 0)
    def _():
        e_ref[...] = jnp.zeros_like(e_ref)

    weights = f_ref[0]
    tile = weights.shape[-1]
    window = 2 * tile
    lanes = e_ref.shape[-1]
    rows_in = offset
    for step in range(steps):
        toep_real = toeplitz_rows(weights[step, 0:1], window)
        toep_imag = toeplitz_rows(weights[step, 1:2], window)
        from_real = jnp.concatenate([toep_real, toep_imag], axis=0).astype(jnp.bfloat16)
        from_imag = jnp.concatenate([-toep_imag, toep_real], axis=0).astype(jnp.bfloat16)
        for q in range(rows_in // tile - 1):
            start = q * tile
            acc = jnp.dot(
                from_real, re_s[start : start + window], preferred_element_type=jnp.float32
            )
            acc = acc + jnp.dot(
                from_imag, im_s[start : start + window], preferred_element_type=jnp.float32
            )
            real_part = acc[:tile]
            imag_part = acc[tile:]
            if step < steps - 1:
                re_t, im_t = turn_rows(
                    real_part.astype(jnp.bfloat16), imag_part.astype(jnp.bfloat16),
                    cos_all[step + 1], sin_all[step + 1],
                )
                re_s[start : start + tile] = re_t
                im_s[start : start + tile] = im_t
            else:
                o_ref[0, start : start + tile] = real_part
                o_ref[1, start : start + tile] = imag_part
                power = real_part * real_part + imag_part * imag_part
                folded = power[:, :lanes]
                for k in range(1, power.shape[1] // lanes):
                    folded = folded + power[:, k * lanes : (k + 1) * lanes]
                e_ref[start : start + tile] += folded
        rows_in -= tile


def compress_all(pieces, offsets, angles, angle_offset, weights, bins):
    blocks = weights.shape[0]
    width = blocks * bins
    rows = sum(piece.shape[1] for piece in pieces)
    steps = angles.shape[0]
    period = angles.shape[1]
    out_rows = rows - steps * weights.shape[-1]
    lanes = 128
    return pl.pallas_call(
        fused_kernel,
        grid=(blocks,),
        in_specs=[
            pl.BlockSpec((2, piece.shape[1], bins), lambda b, o=offset: (0, 0, b + o))
            for piece, offset in zip(pieces, offsets)
        ]
        + [
            pl.BlockSpec((steps, period, bins), lambda b: (0, 0, b + angle_offset)),
            pl.BlockSpec((1,) + weights.shape[1:], lambda b: (b, 0, 0, 0)),
        ],
        out_specs=[
            pl.BlockSpec((2, out_rows, bins), lambda b: (0, 0, b)),
            pl.BlockSpec((out_rows, lanes), lambda b: (0, 0)),
        ],
        out_shape=[
            jax.ShapeDtypeStruct((2, out_rows, width), jnp.float32),
            jax.ShapeDtypeStruct((out_rows, lanes), jnp.float32),
        ],
        scratch_shapes=[
            pltpu.VMEM((rows, bins), jnp.bfloat16),
            pltpu.VMEM((rows, bins), jnp.bfloat16),
        ],
        compiler_params=pltpu.CompilerParams(dimension_semantics=("arbitrary",)),
    )(*pieces, angles, weights)


def on_device(echo, nav_angles, owner, taps, band):
    filters = jnp.transpose(make_taps(taps, band).astype(jnp.float32), (1, 0, 2, 3))
    step_count = taps.shape[0]
    own = jnp.transpose(echo, (1, 0, 2))
    reach = step_count * (taps.shape[-1] // 2)
    assert reach == own.shape[1]
    blocks = filters.shape[0]
    half = blocks * 5 // 8
    bins = own.shape[2] // blocks
    cut = bins * half
    left_a, right_a = exchange(own[:, :, :cut], own[:, :, :cut], "sector")
    mine, _, shapes = from_roots(
        nav_angles, "sector", [owner[step] for step in range(step_count)], own
    )
    all_angles = gather_roots(mine, "sector", shapes)
    own_b, left_a, right_a, all_angles = lax.optimization_barrier(
        (own[:, :, cut:], left_a, right_a, all_angles)
    )
    left_b, right_b = exchange(own_b, own_b, "sector")
    result_a, partial_a = compress_all(
        [left_a, own, right_a], (0, 0, 0), all_angles, 0, filters[:half], bins
    )
    result_b, partial_b = compress_all(
        [left_b, own, right_b], (0, half, 0), all_angles, half, filters[half:], bins
    )
    result = jnp.concatenate([result_a, result_b], axis=2)
    partial = partial_a + partial_b
    energy = lax.psum(jnp.sum(partial, axis=1), "range")
    row_scale = lax.rsqrt(energy / (2.0 * RANGE) + 1e-05)
    scaled = (result * row_scale[None, :, None]).astype(jnp.bfloat16)
    return jnp.transpose(scaled, (1, 0, 2))


def solution(mesh):
    placed = (
        P("sector", None, "range"),
        P("sector", "range"),
        P(),
        P(None, "range", None, None),
        P("range"),
    )
    return jax.shard_map(
        on_device, mesh=mesh, in_specs=placed, out_specs=P("sector", None, "range"), check_vma=False
    )
```

```python
import functools

import jax
import jax.numpy as jnp
from jax import lax
from jax.experimental import pallas as pl
from jax.experimental.pallas import tpu as pltpu
from jax.sharding import PartitionSpec as P

RANGE = 8192


def from_roots(value, axis, sources, tied):
    count = lax.axis_size(axis)
    me = lax.axis_index(axis)
    kept = jnp.stack([jnp.where(me == source, value, 0) for source in sources]).astype(jnp.bfloat16)
    flat = kept.reshape(count, -1)
    part = lax.all_to_all(flat, axis, 0, 0, tiled=True)
    mine = jnp.sum(part, axis=0, keepdims=True)
    mine, tied = lax.optimization_barrier((mine, tied))
    return mine, tied, (flat.shape, kept.shape, value.dtype)


def gather_roots(mine, axis, shapes):
    flat_shape, kept_shape, dtype = shapes
    full = lax.all_to_all(jnp.broadcast_to(mine, flat_shape), axis, 0, 0, tiled=True)
    return full.reshape(kept_shape).astype(dtype)


def exchange(low_rows, high_rows, axis):
    count = lax.axis_size(axis)
    forward = [(i, (i + 1) % count) for i in range(count)]
    backward = [((i + 1) % count, i) for i in range(count)]
    low = lax.ppermute(high_rows, axis, forward)
    high = lax.ppermute(low_rows, axis, backward)
    return low, high


def make_taps(taps, band):
    taps_count = taps.shape[-1]
    half_taps = taps_count // 2
    offsets = jnp.arange(taps_count, dtype=jnp.int32) - half_taps
    band_col = band[:, None]
    inside = (offsets[None, :] >= -band_col) & (offsets[None, :] < band_col)
    band_gain = jnp.sqrt(half_taps / band.astype(jnp.float32))
    weighted = (
        taps.astype(jnp.float32)
        * inside[None, :, None, :].astype(jnp.float32)
        * band_gain[None, :, None, None]
    )
    return weighted.astype(jnp.bfloat16)


def turn_rows(re, im, cosine, sine):
    period = cosine.shape[0]
    rows, width = re.shape
    re = re.astype(jnp.float32).reshape(rows // period, period, width)
    im = im.astype(jnp.float32).reshape(rows // period, period, width)
    real_part = re * cosine[None] - im * sine[None]
    imag_part = re * sine[None] + im * cosine[None]
    return (
        real_part.reshape(rows, width).astype(jnp.bfloat16),
        imag_part.reshape(rows, width).astype(jnp.bfloat16),
    )


def toeplitz_rows(weights, window):
    taps = weights.shape[-1]
    base = jnp.concatenate(
        [jnp.broadcast_to(weights, (taps, taps)), jnp.zeros((taps, window - taps), weights.dtype)],
        axis=1,
    )
    return pltpu.roll(base, 0, 1, stride=1, stride_axis=0)


def fused_kernel(left_ref, own_ref, right_ref, a_ref, f_ref, o_ref, e_ref, re_s, im_s):
    angles = a_ref[...]
    cos_all = jnp.cos(angles)
    sin_all = jnp.sin(angles)
    steps = angles.shape[0]
    offset = 0
    for piece in (left_ref, own_ref, right_ref):
        rows = piece.shape[1]
        re_t, im_t = turn_rows(piece[0], piece[1], cos_all[0], sin_all[0])
        re_s[offset : offset + rows] = re_t
        im_s[offset : offset + rows] = im_t
        offset += rows

    @pl.when(pl.program_id(0) == 0)
    def _():
        e_ref[...] = jnp.zeros_like(e_ref)

    weights = f_ref[0]
    tile = weights.shape[-1]
    window = 2 * tile
    lanes = e_ref.shape[-1]
    rows_in = offset
    for step in range(steps):
        toep_real = toeplitz_rows(weights[step, 0:1], window)
        toep_imag = toeplitz_rows(weights[step, 1:2], window)
        from_real = jnp.concatenate([toep_real, toep_imag], axis=0).astype(jnp.bfloat16)
        from_imag = jnp.concatenate([-toep_imag, toep_real], axis=0).astype(jnp.bfloat16)
        for q in range(rows_in // tile - 1):
            start = q * tile
            acc = jnp.dot(
                from_real, re_s[start : start + window], preferred_element_type=jnp.float32
            )
            acc = acc + jnp.dot(
                from_imag, im_s[start : start + window], preferred_element_type=jnp.float32
            )
            real_part = acc[:tile]
            imag_part = acc[tile:]
            if step < steps - 1:
                re_t, im_t = turn_rows(
                    real_part.astype(jnp.bfloat16), imag_part.astype(jnp.bfloat16),
                    cos_all[step + 1], sin_all[step + 1],
                )
                re_s[start : start + tile] = re_t
                im_s[start : start + tile] = im_t
            else:
                o_ref[0, start : start + tile] = real_part
                o_ref[1, start : start + tile] = imag_part
                power = real_part * real_part + imag_part * imag_part
                folded = power[:, :lanes]
                for k in range(1, power.shape[1] // lanes):
                    folded = folded + power[:, k * lanes : (k + 1) * lanes]
                e_ref[start : start + tile] += folded
        rows_in -= tile


def compress_all(pieces, offsets, angles, angle_offset, weights, bins):
    blocks = weights.shape[0]
    width = blocks * bins
    rows = sum(piece.shape[1] for piece in pieces)
    steps = angles.shape[0]
    period = angles.shape[1]
    out_rows = rows - steps * weights.shape[-1]
    lanes = 128
    return pl.pallas_call(
        fused_kernel,
        grid=(blocks,),
        in_specs=[
            pl.BlockSpec((2, piece.shape[1], bins), lambda b, o=offset: (0, 0, b + o))
            for piece, offset in zip(pieces, offsets)
        ]
        + [
            pl.BlockSpec((steps, period, bins), lambda b: (0, 0, b + angle_offset)),
            pl.BlockSpec((1,) + weights.shape[1:], lambda b: (b, 0, 0, 0)),
        ],
        out_specs=[
            pl.BlockSpec((2, out_rows, bins), lambda b: (0, 0, b)),
            pl.BlockSpec((out_rows, lanes), lambda b: (0, 0)),
        ],
        out_shape=[
            jax.ShapeDtypeStruct((2, out_rows, width), jnp.float32),
            jax.ShapeDtypeStruct((out_rows, lanes), jnp.float32),
        ],
        scratch_shapes=[
            pltpu.VMEM((rows, bins), jnp.bfloat16),
            pltpu.VMEM((rows, bins), jnp.bfloat16),
        ],
        compiler_params=pltpu.CompilerParams(dimension_semantics=("arbitrary",)),
    )(*pieces, angles, weights)


def on_device(echo, nav_angles, owner, taps, band):
    filters = jnp.transpose(make_taps(taps, band).astype(jnp.float32), (1, 0, 2, 3))
    step_count = taps.shape[0]
    own = jnp.transpose(echo, (1, 0, 2))
    reach = step_count * (taps.shape[-1] // 2)
    assert reach == own.shape[1]
    blocks = filters.shape[0]
    half = blocks * 7 // 8
    bins = own.shape[2] // blocks
    cut = bins * half
    left_a, right_a = exchange(own[:, :, :cut], own[:, :, :cut], "sector")
    mine, _, shapes = from_roots(
        nav_angles, "sector", [owner[step] for step in range(step_count)], own
    )
    all_angles = gather_roots(mine, "sector", shapes)
    own_b, left_a, right_a, all_angles = lax.optimization_barrier(
        (own[:, :, cut:], left_a, right_a, all_angles)
    )
    left_b, right_b = exchange(own_b, own_b, "sector")
    result_a, partial_a = compress_all(
        [left_a, own, right_a], (0, 0, 0), all_angles, 0, filters[:half], bins
    )
    result_b, partial_b = compress_all(
        [left_b, own, right_b], (0, half, 0), all_angles, half, filters[half:], bins
    )
    result = jnp.concatenate([result_a, result_b], axis=2)
    partial = partial_a + partial_b
    energy = lax.psum(jnp.sum(partial, axis=1), "range")
    row_scale = lax.rsqrt(energy / (2.0 * RANGE) + 1e-05)
    scaled = (result * row_scale[None, :, None]).astype(jnp.bfloat16)
    return jnp.transpose(scaled, (1, 0, 2))


def solution(mesh):
    placed = (
        P("sector", None, "range"),
        P("sector", "range"),
        P(),
        P(None, "range", None, None),
        P("range"),
    )
    return jax.shard_map(
        on_device, mesh=mesh, in_specs=placed, out_specs=P("sector", None, "range"), check_vma=False
    )
```

```python
import functools

import jax
import jax.numpy as jnp
from jax import lax
from jax.experimental import pallas as pl
from jax.experimental.pallas import tpu as pltpu
from jax.sharding import PartitionSpec as P

RANGE = 8192


def from_roots(value, axis, sources, tied):
    count = lax.axis_size(axis)
    me = lax.axis_index(axis)
    kept = jnp.stack([jnp.where(me == source, value, 0) for source in sources]).astype(jnp.bfloat16)
    flat = kept.reshape(count, -1)
    part = lax.all_to_all(flat, axis, 0, 0, tiled=True)
    mine = jnp.sum(part, axis=0, keepdims=True)
    mine, tied = lax.optimization_barrier((mine, tied))
    return mine, tied, (flat.shape, kept.shape, value.dtype)


def gather_roots(mine, axis, shapes):
    flat_shape, kept_shape, dtype = shapes
    full = lax.all_to_all(jnp.broadcast_to(mine, flat_shape), axis, 0, 0, tiled=True)
    return full.reshape(kept_shape).astype(dtype)


def exchange(low_rows, high_rows, axis):
    count = lax.axis_size(axis)
    forward = [(i, (i + 1) % count) for i in range(count)]
    backward = [((i + 1) % count, i) for i in range(count)]
    low = lax.ppermute(high_rows, axis, forward)
    high = lax.ppermute(low_rows, axis, backward)
    return low, high


def make_taps(taps, band):
    taps_count = taps.shape[-1]
    half_taps = taps_count // 2
    offsets = jnp.arange(taps_count, dtype=jnp.int32) - half_taps
    band_col = band[:, None]
    inside = (offsets[None, :] >= -band_col) & (offsets[None, :] < band_col)
    band_gain = jnp.sqrt(half_taps / band.astype(jnp.float32))
    weighted = (
        taps.astype(jnp.float32)
        * inside[None, :, None, :].astype(jnp.float32)
        * band_gain[None, :, None, None]
    )
    return weighted.astype(jnp.bfloat16)


def turn_rows(re, im, cosine, sine):
    period = cosine.shape[0]
    rows, width = re.shape
    re = re.astype(jnp.float32).reshape(rows // period, period, width)
    im = im.astype(jnp.float32).reshape(rows // period, period, width)
    real_part = re * cosine[None] - im * sine[None]
    imag_part = re * sine[None] + im * cosine[None]
    return (
        real_part.reshape(rows, width).astype(jnp.bfloat16),
        imag_part.reshape(rows, width).astype(jnp.bfloat16),
    )


def toeplitz_rows(weights, window):
    taps = weights.shape[-1]
    base = jnp.concatenate(
        [jnp.broadcast_to(weights, (taps, taps)), jnp.zeros((taps, window - taps), weights.dtype)],
        axis=1,
    )
    return pltpu.roll(base, 0, 1, stride=1, stride_axis=0)


def fused_kernel(left_ref, own_ref, right_ref, c_ref, s_ref, f_ref, o_ref, e_ref, re_s, im_s):
    cos_all = c_ref[...]
    sin_all = s_ref[...]
    steps = cos_all.shape[0]
    offset = 0
    for piece in (left_ref, own_ref, right_ref):
        rows = piece.shape[1]
        re_t, im_t = turn_rows(piece[0], piece[1], cos_all[0], sin_all[0])
        re_s[offset : offset + rows] = re_t
        im_s[offset : offset + rows] = im_t
        offset += rows

    @pl.when(pl.program_id(0) == 0)
    def _():
        e_ref[...] = jnp.zeros_like(e_ref)

    weights = f_ref[0]
    tile = weights.shape[-1]
    window = 2 * tile
    lanes = e_ref.shape[-1]
    rows_in = offset
    for step in range(steps):
        toep_real = toeplitz_rows(weights[step, 0:1], window)
        toep_imag = toeplitz_rows(weights[step, 1:2], window)
        from_real = jnp.concatenate([toep_real, toep_imag], axis=0).astype(jnp.bfloat16)
        from_imag = jnp.concatenate([-toep_imag, toep_real], axis=0).astype(jnp.bfloat16)
        for q in range(rows_in // tile - 1):
            start = q * tile
            acc = jnp.dot(
                from_real, re_s[start : start + window], preferred_element_type=jnp.float32
            )
            acc = acc + jnp.dot(
                from_imag, im_s[start : start + window], preferred_element_type=jnp.float32
            )
            real_part = acc[:tile]
            imag_part = acc[tile:]
            if step < steps - 1:
                re_t, im_t = turn_rows(
                    real_part.astype(jnp.bfloat16), imag_part.astype(jnp.bfloat16),
                    cos_all[step + 1], sin_all[step + 1],
                )
                re_s[start : start + tile] = re_t
                im_s[start : start + tile] = im_t
            else:
                o_ref[0, start : start + tile] = real_part
                o_ref[1, start : start + tile] = imag_part
                power = real_part * real_part + imag_part * imag_part
                folded = power[:, :lanes]
                for k in range(1, power.shape[1] // lanes):
                    folded = folded + power[:, k * lanes : (k + 1) * lanes]
                e_ref[start : start + tile] += folded
        rows_in -= tile


def compress_all(pieces, offsets, angles, angle_offset, weights, bins):
    blocks = weights.shape[0]
    width = blocks * bins
    rows = sum(piece.shape[1] for piece in pieces)
    steps = angles.shape[0]
    period = angles.shape[1]
    out_rows = rows - steps * weights.shape[-1]
    lanes = 128
    return pl.pallas_call(
        fused_kernel,
        grid=(blocks,),
        in_specs=[
            pl.BlockSpec((2, piece.shape[1], bins), lambda b, o=offset: (0, 0, b + o))
            for piece, offset in zip(pieces, offsets)
        ]
        + [
            pl.BlockSpec((steps, period, bins), lambda b: (0, 0, b + angle_offset)),
            pl.BlockSpec((steps, period, bins), lambda b: (0, 0, b + angle_offset)),
            pl.BlockSpec((1,) + weights.shape[1:], lambda b: (b, 0, 0, 0)),
        ],
        out_specs=[
            pl.BlockSpec((2, out_rows, bins), lambda b: (0, 0, b)),
            pl.BlockSpec((out_rows, lanes), lambda b: (0, 0)),
        ],
        out_shape=[
            jax.ShapeDtypeStruct((2, out_rows, width), jnp.float32),
            jax.ShapeDtypeStruct((out_rows, lanes), jnp.float32),
        ],
        scratch_shapes=[
            pltpu.VMEM((rows, bins), jnp.bfloat16),
            pltpu.VMEM((rows, bins), jnp.bfloat16),
        ],
        compiler_params=pltpu.CompilerParams(dimension_semantics=("arbitrary",)),
    )(*pieces, jnp.cos(angles), jnp.sin(angles), weights)


def on_device(echo, nav_angles, owner, taps, band):
    filters = jnp.transpose(make_taps(taps, band).astype(jnp.float32), (1, 0, 2, 3))
    step_count = taps.shape[0]
    own = jnp.transpose(echo, (1, 0, 2))
    reach = step_count * (taps.shape[-1] // 2)
    assert reach == own.shape[1]
    blocks = filters.shape[0]
    half = blocks * 3 // 4
    bins = own.shape[2] // blocks
    cut = bins * half
    left_a, right_a = exchange(own[:, :, :cut], own[:, :, :cut], "sector")
    mine, _, shapes = from_roots(
        nav_angles, "sector", [owner[step] for step in range(step_count)], own
    )
    all_angles = gather_roots(mine, "sector", shapes)
    own_b, left_a, right_a, all_angles = lax.optimization_barrier(
        (own[:, :, cut:], left_a, right_a, all_angles)
    )
    left_b, right_b = exchange(own_b, own_b, "sector")
    result_a, partial_a = compress_all(
        [left_a, own, right_a], (0, 0, 0), all_angles, 0, filters[:half], bins
    )
    result_b, partial_b = compress_all(
        [left_b, own, right_b], (0, half, 0), all_angles, half, filters[half:], bins
    )
    result = jnp.concatenate([result_a, result_b], axis=2)
    partial = partial_a + partial_b
    energy = lax.psum(jnp.sum(partial, axis=1), "range")
    row_scale = lax.rsqrt(energy / (2.0 * RANGE) + 1e-05)
    scaled = (result * row_scale[None, :, None]).astype(jnp.bfloat16)
    return jnp.transpose(scaled, (1, 0, 2))


def solution(mesh):
    placed = (
        P("sector", None, "range"),
        P("sector", "range"),
        P(),
        P(None, "range", None, None),
        P("range"),
    )
    return jax.shard_map(
        on_device, mesh=mesh, in_specs=placed, out_specs=P("sector", None, "range"), check_vma=False
    )
```

```python
import functools

import jax
import jax.numpy as jnp
from jax import lax
from jax.experimental import pallas as pl
from jax.experimental.pallas import tpu as pltpu
from jax.sharding import PartitionSpec as P

RANGE = 8192


def from_roots(value, axis, sources, tied):
    count = lax.axis_size(axis)
    me = lax.axis_index(axis)
    kept = jnp.stack([jnp.where(me == source, value, 0) for source in sources]).astype(jnp.bfloat16)
    flat = kept.reshape(count, -1)
    part = lax.all_to_all(flat, axis, 0, 0, tiled=True)
    mine = jnp.sum(part, axis=0, keepdims=True)
    mine, tied = lax.optimization_barrier((mine, tied))
    return mine, tied, (flat.shape, kept.shape, value.dtype)


def gather_roots(mine, axis, shapes):
    flat_shape, kept_shape, dtype = shapes
    full = lax.all_to_all(jnp.broadcast_to(mine, flat_shape), axis, 0, 0, tiled=True)
    return full.reshape(kept_shape).astype(dtype)


def exchange(low_rows, high_rows, axis):
    count = lax.axis_size(axis)
    forward = [(i, (i + 1) % count) for i in range(count)]
    backward = [((i + 1) % count, i) for i in range(count)]
    low = lax.ppermute(high_rows, axis, forward)
    high = lax.ppermute(low_rows, axis, backward)
    return low, high


def make_taps(taps, band):
    taps_count = taps.shape[-1]
    half_taps = taps_count // 2
    offsets = jnp.arange(taps_count, dtype=jnp.int32) - half_taps
    band_col = band[:, None]
    inside = (offsets[None, :] >= -band_col) & (offsets[None, :] < band_col)
    band_gain = jnp.sqrt(half_taps / band.astype(jnp.float32))
    weighted = (
        taps.astype(jnp.float32)
        * inside[None, :, None, :].astype(jnp.float32)
        * band_gain[None, :, None, None]
    )
    return weighted.astype(jnp.bfloat16)


def turn_rows(re, im, cosine, sine):
    period = cosine.shape[0]
    rows, width = re.shape
    re = re.astype(jnp.float32).reshape(rows // period, period, width)
    im = im.astype(jnp.float32).reshape(rows // period, period, width)
    real_part = re * cosine[None] - im * sine[None]
    imag_part = re * sine[None] + im * cosine[None]
    return (
        real_part.reshape(rows, width).astype(jnp.bfloat16),
        imag_part.reshape(rows, width).astype(jnp.bfloat16),
    )


def toeplitz_rows(weights, window):
    taps = weights.shape[-1]
    base = jnp.concatenate(
        [jnp.broadcast_to(weights, (taps, taps)), jnp.zeros((taps, window - taps), weights.dtype)],
        axis=1,
    )
    return pltpu.roll(base, 0, 1, stride=1, stride_axis=0)


def fused_kernel(left_ref, own_ref, right_ref, a_ref, f_ref, o_ref, e_ref, re_s, im_s):
    angles = a_ref[...]
    cos_all = jnp.cos(angles)
    sin_all = jnp.sin(angles)
    steps = angles.shape[0]
    offset = 0
    for piece in (left_ref, own_ref, right_ref):
        rows = piece.shape[1]
        re_t, im_t = turn_rows(piece[0], piece[1], cos_all[0], sin_all[0])
        re_s[offset : offset + rows] = re_t
        im_s[offset : offset + rows] = im_t
        offset += rows

    @pl.when(pl.program_id(0) == 0)
    def _():
        e_ref[...] = jnp.zeros_like(e_ref)

    weights = f_ref[0]
    tile = weights.shape[-1]
    window = 2 * tile
    lanes = e_ref.shape[-1]
    rows_in = offset
    for step in range(steps):
        toep_real = toeplitz_rows(weights[step, 0:1], window)
        toep_imag = toeplitz_rows(weights[step, 1:2], window)
        from_real = jnp.concatenate([toep_real, toep_imag], axis=0).astype(jnp.bfloat16)
        from_imag = jnp.concatenate([-toep_imag, toep_real], axis=0).astype(jnp.bfloat16)
        for q in range(rows_in // tile - 1):
            start = q * tile
            acc = jnp.dot(
                from_real, re_s[start : start + window], preferred_element_type=jnp.float32
            )
            acc = acc + jnp.dot(
                from_imag, im_s[start : start + window], preferred_element_type=jnp.float32
            )
            real_part = acc[:tile]
            imag_part = acc[tile:]
            if step < steps - 1:
                re_t, im_t = turn_rows(
                    real_part.astype(jnp.bfloat16), imag_part.astype(jnp.bfloat16),
                    cos_all[step + 1], sin_all[step + 1],
                )
                re_s[start : start + tile] = re_t
                im_s[start : start + tile] = im_t
            else:
                o_ref[0, start : start + tile] = real_part
                o_ref[1, start : start + tile] = imag_part
                power = real_part * real_part + imag_part * imag_part
                folded = power[:, :lanes]
                for k in range(1, power.shape[1] // lanes):
                    folded = folded + power[:, k * lanes : (k + 1) * lanes]
                e_ref[start : start + tile] += folded
        rows_in -= tile


def compress_all(pieces, offsets, angles, angle_offset, weights, bins):
    blocks = weights.shape[0]
    width = blocks * bins
    rows = sum(piece.shape[1] for piece in pieces)
    steps = angles.shape[0]
    period = angles.shape[1]
    out_rows = rows - steps * weights.shape[-1]
    lanes = 128
    return pl.pallas_call(
        fused_kernel,
        grid=(blocks,),
        in_specs=[
            pl.BlockSpec((2, piece.shape[1], bins), lambda b, o=offset: (0, 0, b + o))
            for piece, offset in zip(pieces, offsets)
        ]
        + [
            pl.BlockSpec((steps, period, bins), lambda b: (0, 0, b + angle_offset)),
            pl.BlockSpec((1,) + weights.shape[1:], lambda b: (b, 0, 0, 0)),
        ],
        out_specs=[
            pl.BlockSpec((2, out_rows, bins), lambda b: (0, 0, b)),
            pl.BlockSpec((out_rows, lanes), lambda b: (0, 0)),
        ],
        out_shape=[
            jax.ShapeDtypeStruct((2, out_rows, width), jnp.float32),
            jax.ShapeDtypeStruct((out_rows, lanes), jnp.float32),
        ],
        scratch_shapes=[
            pltpu.VMEM((rows, bins), jnp.bfloat16),
            pltpu.VMEM((rows, bins), jnp.bfloat16),
        ],
        compiler_params=pltpu.CompilerParams(dimension_semantics=("arbitrary",)),
    )(*pieces, angles, weights)


def on_device(echo, nav_angles, owner, taps, band):
    filters = jnp.transpose(make_taps(taps, band).astype(jnp.float32), (1, 0, 2, 3))
    step_count = taps.shape[0]
    own = jnp.transpose(echo, (1, 0, 2))
    reach = step_count * (taps.shape[-1] // 2)
    assert reach == own.shape[1]
    blocks = filters.shape[0]
    half = blocks * 3 // 4
    bins = own.shape[2] // blocks
    cut = bins * half
    left_a, right_a = exchange(own[:, :, :cut], own[:, :, :cut], "sector")
    mine, _, shapes = from_roots(
        nav_angles, "sector", [owner[step] for step in range(step_count)], own
    )
    all_angles = gather_roots(mine, "sector", shapes)
    own_b, left_a, right_a = lax.optimization_barrier((own[:, :, cut:], left_a, right_a))
    left_b, right_b = exchange(own_b, own_b, "sector")
    result_a, partial_a = compress_all(
        [left_a, own, right_a], (0, 0, 0), all_angles, 0, filters[:half], bins
    )
    result_b, partial_b = compress_all(
        [left_b, own, right_b], (0, half, 0), all_angles, half, filters[half:], bins
    )
    result = jnp.concatenate([result_a, result_b], axis=2)
    partial = partial_a + partial_b
    energy = lax.psum(jnp.sum(partial, axis=1), "range")
    row_scale = lax.rsqrt(energy / (2.0 * RANGE) + 1e-05)
    scaled = (result * row_scale[None, :, None]).astype(jnp.bfloat16)
    return jnp.transpose(scaled, (1, 0, 2))


def solution(mesh):
    placed = (
        P("sector", None, "range"),
        P("sector", "range"),
        P(),
        P(None, "range", None, None),
        P("range"),
    )
    return jax.shard_map(
        on_device, mesh=mesh, in_specs=placed, out_specs=P("sector", None, "range"), check_vma=False
    )
```
